32 devices in a mesh: seq: 8 (over z, core), head: 4 (over y, x).
Axes of the slice: x: 2, y: 2, z: 4, core: 2. Of those that a mesh axis runs over, the one named last changes fastest.
Arguments:
- conv_output: bfloat16 [1024, 2048], P('seq', 'head'), may hold values from -6 to 6
- output_grad: bfloat16 [1024, 2048], P('seq', 'head'), may hold values from -6 to 6
- write_keys: bfloat16 [1024, 512], P('seq', 'head'), may hold values from -1.5 to 1.5
- read_queries: bfloat16 [1024, 512], P('seq', 'head'), may hold values from -1.5 to 1.5
- log_decay: float32 [1024, 32], P('seq', 'head'), may hold values from -0.7 to 0
- step_size: float32 [1024, 32], P('seq', 'head'), may hold values from 0.005 to 0.05
- skip_gain: float32 [32], P('head'), may hold values from 0.5 to 1.5
- conv_weight: float32 [4, 2048], P(None, 'head'), may hold values from -3 to 3
Outputs:
- input_grad: bfloat16 [1024, 2048], P('seq', 'head')
- keys_grad: float32 [1024, 512], P('seq', 'head')
- queries_grad: float32 [1024, 512], P('seq', 'head')
- decay_grad: float32 [1024, 32], P('seq', 'head')
- step_grad: float32 [1024, 32], P('seq', 'head')
The draws below stay inside these ranges and needn't reach their ends.
All inputs are finite; a program needn't handle non-finite values.
Results may differ from the reference program's by a relative error of at most 0.0055.
Values may be sent and summed in bfloat16 or wider, within the bound.
No kernel may reach another device: no remote copies, remote signals or barrier semaphores. Data moves between devices by JAX's collectives and lax.ppermute only.
A program may use at most 64 MiB of HBM per device.

```python
import math
import jax
import jax.numpy as jnp
from jax import lax

P_SIZE = 64
N = 256
HD = 8
TOK_DEV = 128
HEAD_TOTAL = 32
GROUPS = 2
TOKEN_TOTAL = 1024


def draw_log_decay(key, part):
    random_keys = jax.random.split(key, 7)
    percent = 50
    fast_head = jax.random.randint(random_keys[0], (HEAD_TOTAL,), 0, 100) < percent
    fast_rate = jnp.exp(jax.random.uniform(random_keys[1], (HEAD_TOTAL,), jnp.float32, math.log(1.0 / 50.0), math.log(1.0 / 30.0)))
    slow_rate = jax.random.uniform(random_keys[2], (HEAD_TOTAL,), jnp.float32, 0.1, 0.3) / TOKEN_TOTAL
    head_decay_rate = jnp.where(fast_head, fast_rate, slow_rate)
    blocks = TOKEN_TOTAL // TOK_DEV
    multiplier = jnp.exp(jax.random.uniform(random_keys[3], (blocks, 1, HEAD_TOTAL), jnp.float32, 0.0, math.log(2.0)))
    multiplier = jnp.broadcast_to(multiplier, (blocks, TOK_DEV, HEAD_TOTAL)).reshape(TOKEN_TOTAL, HEAD_TOTAL)
    small_noise = jax.random.uniform(random_keys[4], (TOKEN_TOTAL, HEAD_TOTAL), jnp.float32, 0.5, 1.5)
    spike_mask = jax.random.randint(random_keys[5], (TOKEN_TOTAL, HEAD_TOTAL), 0, max(TOKEN_TOTAL // 2, 1)) == 0
    spike_loss = jax.random.uniform(random_keys[6], (TOKEN_TOTAL, HEAD_TOTAL), jnp.float32, 0.2, 0.4)
    return -head_decay_rate[None, :] * multiplier * small_noise + jnp.where(spike_mask, jnp.log(1.0 - spike_loss), 0.0)


def block_scale(own_key, shape, cuts, smallest, top_value):
    def one(axis_at, parts):
        draws = jax.random.uniform(jax.random.fold_in(jax.random.fold_in(own_key, 6), axis_at), (parts,), jnp.float32, smallest / len(cuts), top_value / len(cuts))
        return jnp.repeat(jnp.exp(draws), shape[axis_at] // parts).reshape((-1,) + (1,) * (len(shape) - axis_at - 1))

    gain = one(*cuts[0])
    for cut in cuts[1:]:
        gain = gain * one(*cut)
    return gain


def noise(stream_key, dims, deviation, most, shards=(), kind=jnp.bfloat16):
    level = block_scale(stream_key, dims, shards, -0.22, 0.18) if shards else 1.0
    array = jax.random.normal(stream_key, dims, jnp.float32) * deviation * level
    return jnp.minimum(jnp.maximum(array, -most), most).astype(kind)


def setup_inputs(seed: int = 0) -> dict:
    splits = jax.random.split(jax.random.key(seed), 9)
    return {
        "conv_output": noise(splits[0], (TOKEN_TOTAL, HEAD_TOTAL * P_SIZE), 1.0, 6.0, ((0, 8), (1, 4))),
        "output_grad": noise(splits[1], (TOKEN_TOTAL, HEAD_TOTAL * P_SIZE), 1.0, 6.0, ((0, 8), (1, 4))),
        "write_keys": noise(splits[2], (TOKEN_TOTAL, GROUPS * N), 0.25, 1.5, ((0, 8), (1, 4))),
        "read_queries": noise(splits[3], (TOKEN_TOTAL, GROUPS * N), 0.25, 1.5, ((0, 8), (1, 4))),
        "log_decay": draw_log_decay(jax.random.fold_in(splits[8], 71), 0),
        "step_size": jnp.clip(jnp.exp(math.log(0.05) - 2.3025851 * jax.random.uniform(splits[5], (TOKEN_TOTAL, HEAD_TOTAL), jnp.float32) ** block_scale(splits[5], (TOKEN_TOTAL, HEAD_TOTAL), ((0, 8), (1, 4)), -0.2, 0.2)), 0.005, 0.05),
        "skip_gain": jnp.clip(0.5 + 1.0 * jax.random.uniform(splits[6], (HEAD_TOTAL,), jnp.float32) ** block_scale(splits[6], (HEAD_TOTAL,), ((0, 4),), -0.2, 0.2), 0.5, 1.5),
        "conv_weight": noise(splits[7], (4, HEAD_TOTAL * P_SIZE), 0.5, 3.0, ((1, 4),), jnp.float32),
    }


precise = lax.Precision.HIGHEST

def group_forward(conv_part, keys_part, queries_part, decay_part, step_part, skip_part, block):
    count = decay_part.shape[1]
    values = jax.nn.silu(conv_part).reshape(-1, block, count, P_SIZE)
    keys_blocks = keys_part.reshape(-1, block, N)
    query_blocks = queries_part.reshape(-1, block, N)
    cumulative = jnp.cumsum(decay_part.reshape(-1, block, count), axis=1)
    step_blocks = step_part.reshape(-1, block, count)
    row_ids = lax.broadcasted_iota(jnp.int32, (block, block), 0)
    col_ids = lax.broadcasted_iota(jnp.int32, (block, block), 1)
    causal = row_ids >= col_ids

    def advance(state, inputs):
        block_values, block_keys, block_queries, block_cum, block_step = inputs
        scores = jnp.dot(block_queries, block_keys.T, precision=precise, preferred_element_type=jnp.float32)
        log_gap = jnp.where(causal[:, :, None], block_cum[:, None, :] - block_cum[None, :, :], -1e+30)
        mixing = jnp.exp(log_gap) * scores[:, :, None] * block_step[None, :, :]
        inside = jnp.einsum('tsh,shp->thp', mixing, block_values, precision=precise)
        carried = jnp.exp(block_cum)[:, :, None] * jnp.einsum('tn,hnp->thp', block_queries, state, precision=precise)
        outputs = inside + carried + skip_part[None, :, None] * block_values
        to_end = jnp.exp(block_cum[-1][None, :] - block_cum) * block_step
        written = jnp.einsum('sn,shp->hnp', block_keys, block_values * to_end[:, :, None], precision=precise)
        new_state = jnp.exp(block_cum[-1])[:, None, None] * state + written
        return (new_state, outputs)
    initial = jnp.zeros((count, N, P_SIZE), conv_part.dtype)
    _, outputs = lax.scan(advance, initial, (values, keys_blocks, query_blocks, cumulative, step_blocks))
    return outputs.reshape(TOKEN_TOTAL, count * P_SIZE)

def reference(conv_output, output_grad, write_keys, read_queries, log_decay, step_size, skip_gain, conv_weight):
    group_heads = 2 * HD
    groups = HEAD_TOTAL // group_heads
    block = math.gcd(TOKEN_TOTAL, 64)
    conv_all = conv_output.astype(jnp.float32).reshape(TOKEN_TOTAL, groups, group_heads * P_SIZE).transpose(1, 0, 2)
    grads_all = output_grad.astype(jnp.float32).reshape(TOKEN_TOTAL, groups, group_heads * P_SIZE).transpose(1, 0, 2)
    keys_all = write_keys.astype(jnp.float32).reshape(TOKEN_TOTAL, groups, N).transpose(1, 0, 2)
    queries_all = read_queries.astype(jnp.float32).reshape(TOKEN_TOTAL, groups, N).transpose(1, 0, 2)
    decay_all = log_decay.reshape(TOKEN_TOTAL, groups, group_heads).transpose(1, 0, 2)
    step_all = step_size.reshape(TOKEN_TOTAL, groups, group_heads).transpose(1, 0, 2)
    skip_all = skip_gain.reshape(groups, group_heads)
    weight_all = conv_weight.reshape(4, groups, group_heads * P_SIZE).transpose(1, 0, 2)

    def one_group(inputs):
        conv_part, grad_part, keys_part, queries_part, decay_part, step_part, skip_part, weight_part = inputs

        def forward(conv_in, keys_in, queries_in, decay_in, step_in):
            return group_forward(conv_in, keys_in, queries_in, decay_in, step_in, skip_part, block)
        _, pullback = jax.vjp(forward, conv_part, keys_part, queries_part, decay_part, step_part)
        conv_grad, keys_grad, queries_grad, decay_grad, step_grad = pullback(grad_part)
        extended = jnp.concatenate([conv_grad, jnp.zeros((3, conv_grad.shape[1]), conv_grad.dtype)], 0)
        input_grad = jnp.zeros_like(conv_grad)
        for offset in range(4):
            input_grad = input_grad + weight_part[offset][None, :] * extended[3 - offset:3 - offset + TOKEN_TOTAL]
        return (input_grad.astype(jnp.bfloat16), keys_grad, queries_grad, decay_grad, step_grad)
    results = lax.map(one_group, (conv_all, grads_all, keys_all, queries_all, decay_all, step_all, skip_all, weight_all))
    input_grad = results[0].transpose(1, 0, 2).reshape(TOKEN_TOTAL, HEAD_TOTAL * P_SIZE)
    keys_grad = results[1].transpose(1, 0, 2).reshape(TOKEN_TOTAL, groups * N)
    queries_grad = results[2].transpose(1, 0, 2).reshape(TOKEN_TOTAL, groups * N)
    decay_grad = results[3].transpose(1, 0, 2).reshape(TOKEN_TOTAL, HEAD_TOTAL)
    step_grad = results[4].transpose(1, 0, 2).reshape(TOKEN_TOTAL, HEAD_TOTAL)
    return (input_grad, keys_grad, queries_grad, decay_grad, step_grad)
```

```python
import jax
import jax.numpy as jnp
from jax import lax
from jax.sharding import PartitionSpec as P

precise = lax.Precision.HIGHEST


def swapped(block, axis, bit):
    count = lax.axis_size(axis)
    route = []
    for low in range(count):
        high = low | 1 << bit
        if high != low and high < count:
            route += [(low, high), (high, low)]
    return lax.ppermute(block, axis, route)


def scanned_in(shards, axis):
    peers = lax.axis_size(axis)
    near = [(jnp.ones_like(a), jnp.zeros_like(s)) for a, s, _ in shards]
    window = [(a, s) for a, s, _ in shards]
    distance = 1
    while distance < peers:
        routes = []
        for _, _, reverse in shards:
            step = -distance if reverse else distance
            routes.append([(i, i + step) for i in range(peers) if 0 <= i + step < peers])
        received = [lax.ppermute(w, axis, r) for w, r in zip(window, routes)]
        more = 2 * distance < peers
        for k, (far_a, far_s) in enumerate(received):
            near_a, near_s = near[k]
            near[k] = (near_a * far_a, near_s + near_a[:, None, None] * far_s)
            if more:
                win_a, win_s = window[k]
                window[k] = (win_a * far_a, win_s + win_a[:, None, None] * far_s)
        distance *= 2
    return [s for _, s in near]


def shifted(block, axis, distance):
    devices = range(lax.axis_size(axis))
    route = [(i - distance, i) for i in devices if i - distance in devices]
    return lax.ppermute(block, axis, route)


def product(left, right):
    return jnp.dot(left, right, preferred_element_type=jnp.float32, precision=precise)


def body(
    conv_output, output_grad, write_keys, read_queries, log_decay, step_size, skip_gain, conv_weight
):
    length = conv_output.shape[0]
    head_count = log_decay.shape[1]
    head_width = conv_output.shape[1] // head_count
    parity = lax.axis_index("head") % 2
    own_first = parity == 0
    partner = swapped((write_keys, read_queries), "head", 0)
    keys_full = jnp.where(
        own_first,
        jnp.concatenate([write_keys, partner[0]], 1),
        jnp.concatenate([partner[0], write_keys], 1),
    ).astype(jnp.float32)
    queries_full = jnp.where(
        own_first,
        jnp.concatenate([read_queries, partner[1]], 1),
        jnp.concatenate([partner[1], read_queries], 1),
    ).astype(jnp.float32)
    state_count = keys_full.shape[1]
    preact = conv_output.astype(jnp.float32)
    values = jax.nn.silu(preact)
    upstream = output_grad.astype(jnp.float32)
    values3 = values.reshape(length, head_count, head_width)
    upstream3 = upstream.reshape(length, head_count, head_width)
    cumulative = jnp.cumsum(log_decay, axis=0)
    totals = cumulative[-1]
    to_end = jnp.exp(totals[None, :] - cumulative)
    from_start = jnp.exp(cumulative)
    weighted = values3 * (to_end * step_size)[:, :, None]
    seeded = upstream3 * from_start[:, :, None]
    local_state = jnp.einsum("ln,lhp->hnp", keys_full, weighted, precision=precise)
    local_grad = jnp.einsum("ln,lhp->hnp", queries_full, seeded, precision=precise)
    decay_total = jnp.exp(totals)
    entering, arriving = scanned_in(
        [(decay_total, local_state, False), (decay_total, local_grad, True)], "seq"
    )
    scores = product(queries_full, keys_full.T)
    row_ids = lax.broadcasted_iota(jnp.int32, (length, length), 0)
    col_ids = lax.broadcasted_iota(jnp.int32, (length, length), 1)
    causal = row_ids >= col_ids
    cum_heads = cumulative.T
    step_heads = step_size.T
    log_gap = jnp.where(causal[None], cum_heads[:, :, None] - cum_heads[:, None, :], -1e30)
    decay_mask = jnp.exp(log_gap)
    pair_dots = jnp.einsum("thp,shp->hts", upstream3, values3, precision=precise)
    masked_scores = decay_mask * scores[None]
    weight_sum = jnp.einsum("hts,hs->ts", decay_mask * pair_dots, step_heads, precision=precise)
    within = jnp.einsum(
        "hts,thp->shp", masked_scores * step_heads[:, None, :], upstream3, precision=precise
    )
    effect = masked_scores * pair_dots
    row_sums = jnp.einsum("hts,hs->th", effect, step_heads, precision=precise)
    col_sums = jnp.sum(effect, 1).T
    from_state = jnp.einsum("ln,hnp->lhp", queries_full, entering, precision=precise)
    into_state = jnp.einsum("ln,hnp->lhp", keys_full, arriving, precision=precise)
    carried = jnp.sum(values3 * into_state, 2)
    step_grad = col_sums + to_end * carried
    value_grad = (
        within
        + skip_gain[None, :, None] * upstream3
        + (to_end * step_size)[:, :, None] * into_state
    )
    leaving = decay_total[:, None, None] * entering + local_state
    decay_terms = (
        row_sums
        - col_sums * step_size
        + from_start * jnp.sum(upstream3 * from_state, 2)
        - to_end * step_size * carried
    )
    last_row = (lax.broadcasted_iota(jnp.int32, (length, 1), 0) == length - 1).astype(jnp.float32)
    decay_terms = decay_terms + last_row * jnp.sum(arriving * leaving, (1, 2))[None, :]
    decay_grad = jnp.flip(jnp.cumsum(jnp.flip(decay_terms, 0), 0), 0)
    query_part = product(weight_sum, keys_full) + jnp.einsum(
        "lhp,hnp->ln", seeded, entering, precision=precise
    )
    key_part = lax.dot_general(
        weight_sum,
        queries_full,
        (((0,), (0,)), ((), ())),
        preferred_element_type=jnp.float32,
        precision=precise,
    )
    key_part = key_part + jnp.einsum("lhp,hnp->ln", weighted, arriving, precision=precise)
    half_width = state_count // 2
    key_mine = jnp.where(own_first, key_part[:, :half_width], key_part[:, half_width:])
    key_other = jnp.where(own_first, key_part[:, half_width:], key_part[:, :half_width])
    query_mine = jnp.where(own_first, query_part[:, :half_width], query_part[:, half_width:])
    query_other = jnp.where(own_first, query_part[:, half_width:], query_part[:, :half_width])
    received = (
        swapped(key_other.astype(jnp.bfloat16), "head", 0).astype(key_other.dtype),
        swapped(query_other.astype(jnp.bfloat16), "head", 0).astype(query_other.dtype),
    )
    keys_grad = key_mine + received[0]
    queries_grad = query_mine + received[1]
    logistic = jax.nn.sigmoid(preact)
    conv_grad = value_grad.reshape(length, -1) * logistic * (1.0 + preact * (1.0 - logistic))
    following = shifted(conv_grad[:3], "seq", -1)
    extended = jnp.concatenate([conv_grad, following], 0)
    input_grad = jnp.zeros_like(conv_grad)
    for offset in range(4):
        input_grad = (
            input_grad + conv_weight[offset][None, :] * extended[3 - offset : 3 - offset + length]
        )
    return (input_grad.astype(jnp.bfloat16), keys_grad, queries_grad, decay_grad, step_grad)


def solution(mesh):
    return jax.shard_map(
        body,
        mesh=mesh,
        in_specs=(
            P("seq", "head"),
            P("seq", "head"),
            P("seq", "head"),
            P("seq", "head"),
            P("seq", "head"),
            P("seq", "head"),
            P("head"),
            P(None, "head"),
        ),
        out_specs=(
            P("seq", "head"),
            P("seq", "head"),
            P("seq", "head"),
            P("seq", "head"),
            P("seq", "head"),
        ),
        check_vma=False,
    )
```

```python
import jax
import jax.numpy as jnp
from jax import lax
from jax.sharding import PartitionSpec as P

precise = lax.Precision.HIGHEST


def swapped(block, axis, bit):
    count = lax.axis_size(axis)
    route = []
    for low in range(count):
        high = low | 1 << bit
        if high != low and high < count:
            route += [(low, high), (high, low)]
    return lax.ppermute(block, axis, route)


def scanned_in(shards, axis):
    peers = lax.axis_size(axis)
    near = [(jnp.ones_like(a), jnp.zeros_like(s)) for a, s, _ in shards]
    window = [(a, s) for a, s, _ in shards]
    distance = 1
    while distance < peers:
        routes = []
        for _, _, reverse in shards:
            step = -distance if reverse else distance
            routes.append([(i, i + step) for i in range(peers) if 0 <= i + step < peers])
        received = [lax.ppermute(w, axis, r) for w, r in zip(window, routes)]
        more = 2 * distance < peers
        for k, (far_a, far_s) in enumerate(received):
            near_a, near_s = near[k]
            near[k] = (near_a * far_a, near_s + near_a[:, None, None] * far_s)
            if more:
                win_a, win_s = window[k]
                window[k] = (win_a * far_a, win_s + win_a[:, None, None] * far_s)
        distance *= 2
    return [s for _, s in near]


def chip_scanned_in(shards, axis):
    peers = lax.axis_size(axis)
    if peers % 2:
        return scanned_in(shards, axis)
    parity = lax.axis_index(axis) % 2
    pairs = [(2 * k, 2 * k + 1) for k in range(peers // 2)]
    results = []
    for own_a, own_s, reverse in shards:
        inward = [(b, a) for a, b in pairs] if reverse else pairs
        heads = [b for _, b in inward]
        mate_a, mate_s = lax.ppermute((own_a, own_s), axis, inward)
        window = (own_a * mate_a, own_s + own_a[:, None, None] * mate_s)
        near = (jnp.ones_like(own_a), jnp.zeros_like(own_s))
        distance = 2
        while distance < peers:
            step = -distance if reverse else distance
            route = [(i, i + step) for i in heads if 0 <= i + step < peers]
            far_a, far_s = lax.ppermute(window, axis, route)
            near = (near[0] * far_a, near[1] + near[0][:, None, None] * far_s)
            if 2 * distance < peers:
                window = (window[0] * far_a, window[1] + window[0][:, None, None] * far_s)
            distance *= 2
        handed = lax.ppermute(near[1], axis, [(b, a) for a, b in inward])
        is_head = parity == (0 if reverse else 1)
        results.append(
            jnp.where(is_head, mate_s + mate_a[:, None, None] * near[1], handed)
        )
    return results


def shifted(block, axis, distance):
    devices = range(lax.axis_size(axis))
    route = [(i - distance, i) for i in devices if i - distance in devices]
    return lax.ppermute(block, axis, route)


def product(left, right):
    return jnp.dot(left, right, preferred_element_type=jnp.float32, precision=precise)


def body(
    conv_output, output_grad, write_keys, read_queries, log_decay, step_size, skip_gain, conv_weight
):
    length = conv_output.shape[0]
    head_count = log_decay.shape[1]
    head_width = conv_output.shape[1] // head_count
    parity = lax.axis_index("head") % 2
    own_first = parity == 0
    partner = swapped((write_keys, read_queries), "head", 0)
    keys_full = jnp.where(
        own_first,
        jnp.concatenate([write_keys, partner[0]], 1),
        jnp.concatenate([partner[0], write_keys], 1),
    ).astype(jnp.float32)
    queries_full = jnp.where(
        own_first,
        jnp.concatenate([read_queries, partner[1]], 1),
        jnp.concatenate([partner[1], read_queries], 1),
    ).astype(jnp.float32)
    state_count = keys_full.shape[1]
    preact = conv_output.astype(jnp.float32)
    values = jax.nn.silu(preact)
    upstream = output_grad.astype(jnp.float32)
    values3 = values.reshape(length, head_count, head_width)
    upstream3 = upstream.reshape(length, head_count, head_width)
    cumulative = jnp.cumsum(log_decay, axis=0)
    totals = cumulative[-1]
    to_end = jnp.exp(totals[None, :] - cumulative)
    from_start = jnp.exp(cumulative)
    weighted = values3 * (to_end * step_size)[:, :, None]
    seeded = upstream3 * from_start[:, :, None]
    local_state = jnp.einsum("ln,lhp->hnp", keys_full, weighted, precision=precise)
    local_grad = jnp.einsum("ln,lhp->hnp", queries_full, seeded, precision=precise)
    decay_total = jnp.exp(totals)
    entering, arriving = chip_scanned_in(
        [(decay_total, local_state, False), (decay_total, local_grad, True)], "seq"
    )
    scores = product(queries_full, keys_full.T)
    row_ids = lax.broadcasted_iota(jnp.int32, (length, length), 0)
    col_ids = lax.broadcasted_iota(jnp.int32, (length, length), 1)
    causal = row_ids >= col_ids
    cum_heads = cumulative.T
    step_heads = step_size.T
    log_gap = jnp.where(causal[None], cum_heads[:, :, None] - cum_heads[:, None, :], -1e30)
    decay_mask = jnp.exp(log_gap)
    pair_dots = jnp.einsum("thp,shp->hts", upstream3, values3, precision=precise)
    masked_scores = decay_mask * scores[None]
    weight_sum = jnp.einsum("hts,hs->ts", decay_mask * pair_dots, step_heads, precision=precise)
    within = jnp.einsum(
        "hts,thp->shp", masked_scores * step_heads[:, None, :], upstream3, precision=precise
    )
    effect = masked_scores * pair_dots
    row_sums = jnp.einsum("hts,hs->th", effect, step_heads, precision=precise)
    col_sums = jnp.sum(effect, 1).T
    from_state = jnp.einsum("ln,hnp->lhp", queries_full, entering, precision=precise)
    into_state = jnp.einsum("ln,hnp->lhp", keys_full, arriving, precision=precise)
    carried = jnp.sum(values3 * into_state, 2)
    step_grad = col_sums + to_end * carried
    value_grad = (
        within
        + skip_gain[None, :, None] * upstream3
        + (to_end * step_size)[:, :, None] * into_state
    )
    leaving = decay_total[:, None, None] * entering + local_state
    decay_terms = (
        row_sums
        - col_sums * step_size
        + from_start * jnp.sum(upstream3 * from_state, 2)
        - to_end * step_size * carried
    )
    last_row = (lax.broadcasted_iota(jnp.int32, (length, 1), 0) == length - 1).astype(jnp.float32)
    decay_terms = decay_terms + last_row * jnp.sum(arriving * leaving, (1, 2))[None, :]
    decay_grad = jnp.flip(jnp.cumsum(jnp.flip(decay_terms, 0), 0), 0)
    query_part = product(weight_sum, keys_full) + jnp.einsum(
        "lhp,hnp->ln", seeded, entering, precision=precise
    )
    key_part = lax.dot_general(
        weight_sum,
        queries_full,
        (((0,), (0,)), ((), ())),
        preferred_element_type=jnp.float32,
        precision=precise,
    )
    key_part = key_part + jnp.einsum("lhp,hnp->ln", weighted, arriving, precision=precise)
    half_width = state_count // 2
    key_mine = jnp.where(own_first, key_part[:, :half_width], key_part[:, half_width:])
    key_other = jnp.where(own_first, key_part[:, half_width:], key_part[:, :half_width])
    query_mine = jnp.where(own_first, query_part[:, :half_width], query_part[:, half_width:])
    query_other = jnp.where(own_first, query_part[:, half_width:], query_part[:, :half_width])
    received = (
        swapped(key_other.astype(jnp.bfloat16), "head", 0).astype(key_other.dtype),
        swapped(query_other.astype(jnp.bfloat16), "head", 0).astype(query_other.dtype),
    )
    keys_grad = key_mine + received[0]
    queries_grad = query_mine + received[1]
    logistic = jax.nn.sigmoid(preact)
    conv_grad = value_grad.reshape(length, -1) * logistic * (1.0 + preact * (1.0 - logistic))
    following = shifted(conv_grad[:3], "seq", -1)
    extended = jnp.concatenate([conv_grad, following], 0)
    input_grad = jnp.zeros_like(conv_grad)
    for offset in range(4):
        input_grad = (
            input_grad + conv_weight[offset][None, :] * extended[3 - offset : 3 - offset + length]
        )
    return (input_grad.astype(jnp.bfloat16), keys_grad, queries_grad, decay_grad, step_grad)


def solution(mesh):
    return jax.shard_map(
        body,
        mesh=mesh,
        in_specs=(
            P("seq", "head"),
            P("seq", "head"),
            P("seq", "head"),
            P("seq", "head"),
            P("seq", "head"),
            P("seq", "head"),
            P("head"),
            P(None, "head"),
        ),
        out_specs=(
            P("seq", "head"),
            P("seq", "head"),
            P("seq", "head"),
            P("seq", "head"),
            P("seq", "head"),
        ),
        check_vma=False,
    )
```

```python
import jax
import jax.numpy as jnp
from jax import lax
from jax.sharding import PartitionSpec as P

precise = lax.Precision.HIGHEST


def swapped(block, axis, bit):
    count = lax.axis_size(axis)
    route = []
    for low in range(count):
        high = low | 1 << bit
        if high != low and high < count:
            route += [(low, high), (high, low)]
    return lax.ppermute(block, axis, route)


def scanned_in(shards, axis):
    peers = lax.axis_size(axis)
    near = [(jnp.ones_like(a), jnp.zeros_like(s)) for a, s, _ in shards]
    window = [(a, s) for a, s, _ in shards]
    distance = 1
    while distance < peers:
        routes = []
        for _, _, reverse in shards:
            step = -distance if reverse else distance
            routes.append([(i, i + step) for i in range(peers) if 0 <= i + step < peers])
        received = [lax.ppermute(w, axis, r) for w, r in zip(window, routes)]
        more = 2 * distance < peers
        for k, (far_a, far_s) in enumerate(received):
            near_a, near_s = near[k]
            near[k] = (near_a * far_a, near_s + near_a[:, None, None] * far_s)
            if more:
                win_a, win_s = window[k]
                window[k] = (win_a * far_a, win_s + win_a[:, None, None] * far_s)
        distance *= 2
    return [s for _, s in near]


def packed(decay, state, kind):
    heads, width = state.shape[0], state.shape[1]
    if kind == jnp.float32:
        parts = decay
    else:
        high = decay.astype(kind)
        parts = jnp.concatenate([high, (decay - high.astype(decay.dtype)).astype(kind)])
    row = jnp.pad(parts.astype(kind), (0, width - parts.shape[0]))
    slab = jnp.broadcast_to(row[None, :, None], (1,) + state.shape[1:])
    return jnp.concatenate([state.astype(kind), slab], 0)


def unpacked(message):
    heads = message.shape[0] - 1
    row = message[heads, :, 0].astype(jnp.float32)
    decay = row[:heads] if message.dtype == jnp.float32 else row[:heads] + row[heads : 2 * heads]
    return decay, message[:heads].astype(jnp.float32)


def chip_scanned_in(shards, axis):
    peers = lax.axis_size(axis)
    if peers % 2:
        return scanned_in(shards, axis)
    parity = lax.axis_index(axis) % 2
    pairs = [(2 * k, 2 * k + 1) for k in range(peers // 2)]
    results = []
    for own_a, own_s, reverse in shards:
        inward = [(b, a) for a, b in pairs] if reverse else pairs
        heads = [b for _, b in inward]
        mate_a, mate_s = unpacked(
            lax.ppermute(packed(own_a, own_s, jnp.float32), axis, inward)
        )
        window = (own_a * mate_a, own_s + own_a[:, None, None] * mate_s)
        near = (jnp.ones_like(own_a), jnp.zeros_like(own_s))
        distance = 2
        while distance < peers:
            step = -distance if reverse else distance
            route = [(i, i + step) for i in heads if 0 <= i + step < peers]
            last = 2 * distance >= peers
            if last:
                far_s = lax.ppermute(window[1].astype(jnp.bfloat16), axis, route)
                far_s = far_s.astype(jnp.float32)
                near = (near[0], near[1] + near[0][:, None, None] * far_s)
            else:
                far_a, far_s = unpacked(
                    lax.ppermute(packed(*window, jnp.bfloat16), axis, route)
                )
                near = (near[0] * far_a, near[1] + near[0][:, None, None] * far_s)
                window = (window[0] * far_a, window[1] + window[0][:, None, None] * far_s)
            distance *= 2
        handed = lax.ppermute(near[1], axis, [(b, a) for a, b in inward])
        is_head = parity == (0 if reverse else 1)
        results.append(
            jnp.where(is_head, mate_s + mate_a[:, None, None] * near[1], handed)
        )
    return results


def shifted(block, axis, distance):
    devices = range(lax.axis_size(axis))
    route = [(i - distance, i) for i in devices if i - distance in devices]
    return lax.ppermute(block, axis, route)


def product(left, right):
    return jnp.dot(left, right, preferred_element_type=jnp.float32, precision=precise)


def body(
    conv_output, output_grad, write_keys, read_queries, log_decay, step_size, skip_gain, conv_weight
):
    length = conv_output.shape[0]
    head_count = log_decay.shape[1]
    head_width = conv_output.shape[1] // head_count
    parity = lax.axis_index("head") % 2
    own_first = parity == 0
    half = write_keys.shape[1]
    both = swapped(jnp.concatenate([write_keys, read_queries], 1), "head", 0)
    partner = (both[:, :half], both[:, half:])
    keys_full = jnp.where(
        own_first,
        jnp.concatenate([write_keys, partner[0]], 1),
        jnp.concatenate([partner[0], write_keys], 1),
    ).astype(jnp.float32)
    queries_full = jnp.where(
        own_first,
        jnp.concatenate([read_queries, partner[1]], 1),
        jnp.concatenate([partner[1], read_queries], 1),
    ).astype(jnp.float32)
    state_count = keys_full.shape[1]
    preact = conv_output.astype(jnp.float32)
    values = jax.nn.silu(preact)
    upstream = output_grad.astype(jnp.float32)
    values3 = values.reshape(length, head_count, head_width)
    upstream3 = upstream.reshape(length, head_count, head_width)
    cumulative = jnp.cumsum(log_decay, axis=0)
    totals = cumulative[-1]
    to_end = jnp.exp(totals[None, :] - cumulative)
    from_start = jnp.exp(cumulative)
    weighted = values3 * (to_end * step_size)[:, :, None]
    seeded = upstream3 * from_start[:, :, None]
    local_state = jnp.einsum("ln,lhp->hnp", keys_full, weighted, precision=precise)
    local_grad = jnp.einsum("ln,lhp->hnp", queries_full, seeded, precision=precise)
    decay_total = jnp.exp(totals)
    entering, arriving = chip_scanned_in(
        [(decay_total, local_state, False), (decay_total, local_grad, True)], "seq"
    )
    scores = product(queries_full, keys_full.T)
    row_ids = lax.broadcasted_iota(jnp.int32, (length, length), 0)
    col_ids = lax.broadcasted_iota(jnp.int32, (length, length), 1)
    causal = row_ids >= col_ids
    cum_heads = cumulative.T
    step_heads = step_size.T
    log_gap = jnp.where(causal[None], cum_heads[:, :, None] - cum_heads[:, None, :], -1e30)
    decay_mask = jnp.exp(log_gap)
    pair_dots = jnp.einsum("thp,shp->hts", upstream3, values3, precision=precise)
    masked_scores = decay_mask * scores[None]
    weight_sum = jnp.einsum("hts,hs->ts", decay_mask * pair_dots, step_heads, precision=precise)
    within = jnp.einsum(
        "hts,thp->shp", masked_scores * step_heads[:, None, :], upstream3, precision=precise
    )
    effect = masked_scores * pair_dots
    row_sums = jnp.einsum("hts,hs->th", effect, step_heads, precision=precise)
    col_sums = jnp.sum(effect, 1).T
    from_state = jnp.einsum("ln,hnp->lhp", queries_full, entering, precision=precise)
    into_state = jnp.einsum("ln,hnp->lhp", keys_full, arriving, precision=precise)
    carried = jnp.sum(values3 * into_state, 2)
    step_grad = col_sums + to_end * carried
    value_grad = (
        within
        + skip_gain[None, :, None] * upstream3
        + (to_end * step_size)[:, :, None] * into_state
    )
    leaving = decay_total[:, None, None] * entering + local_state
    decay_terms = (
        row_sums
        - col_sums * step_size
        + from_start * jnp.sum(upstream3 * from_state, 2)
        - to_end * step_size * carried
    )
    last_row = (lax.broadcasted_iota(jnp.int32, (length, 1), 0) == length - 1).astype(jnp.float32)
    decay_terms = decay_terms + last_row * jnp.sum(arriving * leaving, (1, 2))[None, :]
    decay_grad = jnp.flip(jnp.cumsum(jnp.flip(decay_terms, 0), 0), 0)
    query_part = product(weight_sum, keys_full) + jnp.einsum(
        "lhp,hnp->ln", seeded, entering, precision=precise
    )
    key_part = lax.dot_general(
        weight_sum,
        queries_full,
        (((0,), (0,)), ((), ())),
        preferred_element_type=jnp.float32,
        precision=precise,
    )
    key_part = key_part + jnp.einsum("lhp,hnp->ln", weighted, arriving, precision=precise)
    half_width = state_count // 2
    key_mine = jnp.where(own_first, key_part[:, :half_width], key_part[:, half_width:])
    key_other = jnp.where(own_first, key_part[:, half_width:], key_part[:, :half_width])
    query_mine = jnp.where(own_first, query_part[:, :half_width], query_part[:, half_width:])
    query_other = jnp.where(own_first, query_part[:, half_width:], query_part[:, :half_width])
    sent_back = swapped(
        jnp.concatenate([key_other, query_other], 1).astype(jnp.bfloat16), "head", 0
    ).astype(key_other.dtype)
    received = (sent_back[:, :half_width], sent_back[:, half_width:])
    keys_grad = key_mine + received[0]
    queries_grad = query_mine + received[1]
    logistic = jax.nn.sigmoid(preact)
    conv_grad = value_grad.reshape(length, -1) * logistic * (1.0 + preact * (1.0 - logistic))
    following = shifted(conv_grad[:3], "seq", -1)
    extended = jnp.concatenate([conv_grad, following], 0)
    input_grad = jnp.zeros_like(conv_grad)
    for offset in range(4):
        input_grad = (
            input_grad + conv_weight[offset][None, :] * extended[3 - offset : 3 - offset + length]
        )
    return (input_grad.astype(jnp.bfloat16), keys_grad, queries_grad, decay_grad, step_grad)


def solution(mesh):
    return jax.shard_map(
        body,
        mesh=mesh,
        in_specs=(
            P("seq", "head"),
            P("seq", "head"),
            P("seq", "head"),
            P("seq", "head"),
            P("seq", "head"),
            P("seq", "head"),
            P("head"),
            P(None, "head"),
        ),
        out_specs=(
            P("seq", "head"),
            P("seq", "head"),
            P("seq", "head"),
            P("seq", "head"),
            P("seq", "head"),
        ),
        check_vma=False,
    )
```

```python
import jax
import jax.numpy as jnp
from jax import lax
from jax.sharding import PartitionSpec as P

precise = lax.Precision.HIGHEST


def swapped(block, axis, bit):
    count = lax.axis_size(axis)
    route = []
    for low in range(count):
        high = low | 1 << bit
        if high != low and high < count:
            route += [(low, high), (high, low)]
    return lax.ppermute(block, axis, route)


def scanned_in(shards, axis):
    peers = lax.axis_size(axis)
    near = [(jnp.ones_like(a), jnp.zeros_like(s)) for a, s, _ in shards]
    window = [(a, s) for a, s, _ in shards]
    distance = 1
    while distance < peers:
        routes = []
        for _, _, reverse in shards:
            step = -distance if reverse else distance
            routes.append([(i, i + step) for i in range(peers) if 0 <= i + step < peers])
        received = [lax.ppermute(w, axis, r) for w, r in zip(window, routes)]
        more = 2 * distance < peers
        for k, (far_a, far_s) in enumerate(received):
            near_a, near_s = near[k]
            near[k] = (near_a * far_a, near_s + near_a[:, None, None] * far_s)
            if more:
                win_a, win_s = window[k]
                window[k] = (win_a * far_a, win_s + win_a[:, None, None] * far_s)
        distance *= 2
    return [s for _, s in near]


def packed(decay, state, kind):
    heads, width = state.shape[0], state.shape[1]
    if kind == jnp.float32:
        parts = decay
    else:
        high = decay.astype(kind)
        parts = jnp.concatenate([high, (decay - high.astype(decay.dtype)).astype(kind)])
    row = jnp.pad(parts.astype(kind), (0, width - parts.shape[0]))
    slab = jnp.broadcast_to(row[None, :, None], (1,) + state.shape[1:])
    return jnp.concatenate([state.astype(kind), slab], 0)


def unpacked(message):
    heads = message.shape[0] - 1
    row = message[heads, :, 0].astype(jnp.float32)
    decay = row[:heads] if message.dtype == jnp.float32 else row[:heads] + row[heads : 2 * heads]
    return decay, message[:heads].astype(jnp.float32)


def paired_scan(decay, state, state_grad, axis):
    peers = lax.axis_size(axis)
    if peers % 2:
        return scanned_in([(decay, state, False), (decay, state_grad, True)], axis)
    is_odd = lax.axis_index(axis) % 2 == 1
    swap = [(i, i ^ 1) for i in range(peers)]
    sent = jnp.where(is_odd, state_grad, state)
    mate_a, mate_s = unpacked(lax.ppermute(packed(decay, sent, jnp.float32), axis, swap))
    own = jnp.where(is_odd, state, state_grad)
    window = (decay * mate_a, own + decay[:, None, None] * mate_s)
    near = (jnp.ones_like(decay), jnp.zeros_like(own))
    distance = 2
    while distance < peers:
        route = [(i, i + distance) for i in range(1, peers, 2) if i + distance < peers]
        route += [(i, i - distance) for i in range(0, peers, 2) if i - distance >= 0]
        if 2 * distance >= peers:
            far_s = lax.ppermute(window[1].astype(jnp.bfloat16), axis, route)
            near = (near[0], near[1] + near[0][:, None, None] * far_s.astype(jnp.float32))
        else:
            far_a, far_s = unpacked(lax.ppermute(packed(*window, jnp.bfloat16), axis, route))
            near = (near[0] * far_a, near[1] + near[0][:, None, None] * far_s)
            window = (window[0] * far_a, window[1] + window[0][:, None, None] * far_s)
        distance *= 2
    handed = lax.ppermute(near[1], axis, swap)
    mine = mate_s + mate_a[:, None, None] * near[1]
    return jnp.where(is_odd, mine, handed), jnp.where(is_odd, handed, mine)


def shifted(block, axis, distance):
    devices = range(lax.axis_size(axis))
    route = [(i - distance, i) for i in devices if i - distance in devices]
    return lax.ppermute(block, axis, route)


def product(left, right):
    return jnp.dot(left, right, preferred_element_type=jnp.float32, precision=precise)


def body(
    conv_output, output_grad, write_keys, read_queries, log_decay, step_size, skip_gain, conv_weight
):
    length = conv_output.shape[0]
    head_count = log_decay.shape[1]
    head_width = conv_output.shape[1] // head_count
    parity = lax.axis_index("head") % 2
    own_first = parity == 0
    half = write_keys.shape[1]
    both = swapped(jnp.concatenate([write_keys, read_queries], 1), "head", 0)
    partner = (both[:, :half], both[:, half:])
    keys_full = jnp.where(
        own_first,
        jnp.concatenate([write_keys, partner[0]], 1),
        jnp.concatenate([partner[0], write_keys], 1),
    ).astype(jnp.float32)
    queries_full = jnp.where(
        own_first,
        jnp.concatenate([read_queries, partner[1]], 1),
        jnp.concatenate([partner[1], read_queries], 1),
    ).astype(jnp.float32)
    state_count = keys_full.shape[1]
    preact = conv_output.astype(jnp.float32)
    values = jax.nn.silu(preact)
    upstream = output_grad.astype(jnp.float32)
    values3 = values.reshape(length, head_count, head_width)
    upstream3 = upstream.reshape(length, head_count, head_width)
    cumulative = jnp.cumsum(log_decay, axis=0)
    totals = cumulative[-1]
    to_end = jnp.exp(totals[None, :] - cumulative)
    from_start = jnp.exp(cumulative)
    weighted = values3 * (to_end * step_size)[:, :, None]
    seeded = upstream3 * from_start[:, :, None]
    local_state = jnp.einsum("ln,lhp->hnp", keys_full, weighted, precision=precise)
    local_grad = jnp.einsum("ln,lhp->hnp", queries_full, seeded, precision=precise)
    decay_total = jnp.exp(totals)
    entering, arriving = paired_scan(decay_total, local_state, local_grad, "seq")
    scores = product(queries_full, keys_full.T)
    row_ids = lax.broadcasted_iota(jnp.int32, (length, length), 0)
    col_ids = lax.broadcasted_iota(jnp.int32, (length, length), 1)
    causal = row_ids >= col_ids
    cum_heads = cumulative.T
    step_heads = step_size.T
    log_gap = jnp.where(causal[None], cum_heads[:, :, None] - cum_heads[:, None, :], -1e30)
    decay_mask = jnp.exp(log_gap)
    pair_dots = jnp.einsum("thp,shp->hts", upstream3, values3, precision=precise)
    masked_scores = decay_mask * scores[None]
    weight_sum = jnp.einsum("hts,hs->ts", decay_mask * pair_dots, step_heads, precision=precise)
    within = jnp.einsum(
        "hts,thp->shp", masked_scores * step_heads[:, None, :], upstream3, precision=precise
    )
    effect = masked_scores * pair_dots
    row_sums = jnp.einsum("hts,hs->th", effect, step_heads, precision=precise)
    col_sums = jnp.sum(effect, 1).T
    from_state = jnp.einsum("ln,hnp->lhp", queries_full, entering, precision=precise)
    into_state = jnp.einsum("ln,hnp->lhp", keys_full, arriving, precision=precise)
    carried = jnp.sum(values3 * into_state, 2)
    step_grad = col_sums + to_end * carried
    value_grad = (
        within
        + skip_gain[None, :, None] * upstream3
        + (to_end * step_size)[:, :, None] * into_state
    )
    leaving = decay_total[:, None, None] * entering + local_state
    decay_terms = (
        row_sums
        - col_sums * step_size
        + from_start * jnp.sum(upstream3 * from_state, 2)
        - to_end * step_size * carried
    )
    last_row = (lax.broadcasted_iota(jnp.int32, (length, 1), 0) == length - 1).astype(jnp.float32)
    decay_terms = decay_terms + last_row * jnp.sum(arriving * leaving, (1, 2))[None, :]
    decay_grad = jnp.flip(jnp.cumsum(jnp.flip(decay_terms, 0), 0), 0)
    query_part = product(weight_sum, keys_full) + jnp.einsum(
        "lhp,hnp->ln", seeded, entering, precision=precise
    )
    key_part = lax.dot_general(
        weight_sum,
        queries_full,
        (((0,), (0,)), ((), ())),
        preferred_element_type=jnp.float32,
        precision=precise,
    )
    key_part = key_part + jnp.einsum("lhp,hnp->ln", weighted, arriving, precision=precise)
    half_width = state_count // 2
    key_mine = jnp.where(own_first, key_part[:, :half_width], key_part[:, half_width:])
    key_other = jnp.where(own_first, key_part[:, half_width:], key_part[:, :half_width])
    query_mine = jnp.where(own_first, query_part[:, :half_width], query_part[:, half_width:])
    query_other = jnp.where(own_first, query_part[:, half_width:], query_part[:, :half_width])
    sent_back = swapped(
        jnp.concatenate([key_other, query_other], 1).astype(jnp.bfloat16), "head", 0
    ).astype(key_other.dtype)
    received = (sent_back[:, :half_width], sent_back[:, half_width:])
    keys_grad = key_mine + received[0]
    queries_grad = query_mine + received[1]
    logistic = jax.nn.sigmoid(preact)
    conv_grad = value_grad.reshape(length, -1) * logistic * (1.0 + preact * (1.0 - logistic))
    following = shifted(conv_grad[:3], "seq", -1)
    extended = jnp.concatenate([conv_grad, following], 0)
    input_grad = jnp.zeros_like(conv_grad)
    for offset in range(4):
        input_grad = (
            input_grad + conv_weight[offset][None, :] * extended[3 - offset : 3 - offset + length]
        )
    return (input_grad.astype(jnp.bfloat16), keys_grad, queries_grad, decay_grad, step_grad)


def solution(mesh):
    return jax.shard_map(
        body,
        mesh=mesh,
        in_specs=(
            P("seq", "head"),
            P("seq", "head"),
            P("seq", "head"),
            P("seq", "head"),
            P("seq", "head"),
            P("seq", "head"),
            P("head"),
            P(None, "head"),
        ),
        out_specs=(
            P("seq", "head"),
            P("seq", "head"),
            P("seq", "head"),
            P("seq", "head"),
            P("seq", "head"),
        ),
        check_vma=False,
    )
```

```python
import jax
import jax.numpy as jnp
from jax import lax
from jax.sharding import PartitionSpec as P

precise = lax.Precision.HIGHEST


def swapped(block, axis, bit):
    count = lax.axis_size(axis)
    route = []
    for low in range(count):
        high = low | 1 << bit
        if high != low and high < count:
            route += [(low, high), (high, low)]
    return lax.ppermute(block, axis, route)


def scanned_in(shards, axis):
    peers = lax.axis_size(axis)
    near = [(jnp.ones_like(a), jnp.zeros_like(s)) for a, s, _ in shards]
    window = [(a, s) for a, s, _ in shards]
    distance = 1
    while distance < peers:
        routes = []
        for _, _, reverse in shards:
            step = -distance if reverse else distance
            routes.append([(i, i + step) for i in range(peers) if 0 <= i + step < peers])
        received = [lax.ppermute(w, axis, r) for w, r in zip(window, routes)]
        more = 2 * distance < peers
        for k, (far_a, far_s) in enumerate(received):
            near_a, near_s = near[k]
            near[k] = (near_a * far_a, near_s + near_a[:, None, None] * far_s)
            if more:
                win_a, win_s = window[k]
                window[k] = (win_a * far_a, win_s + win_a[:, None, None] * far_s)
        distance *= 2
    return [s for _, s in near]


def packed(decay, state, kind):
    heads, width = state.shape[0], state.shape[1]
    if kind == jnp.float32:
        parts = decay
    else:
        high = decay.astype(kind)
        parts = jnp.concatenate([high, (decay - high.astype(decay.dtype)).astype(kind)])
    row = jnp.pad(parts.astype(kind), (0, width - parts.shape[0]))
    slab = jnp.broadcast_to(row[None, :, None], (1,) + state.shape[1:])
    return jnp.concatenate([state.astype(kind), slab], 0)


def unpacked(message):
    heads = message.shape[0] - 1
    row = message[heads, :, 0].astype(jnp.float32)
    decay = row[:heads] if message.dtype == jnp.float32 else row[:heads] + row[heads : 2 * heads]
    return decay, message[:heads].astype(jnp.float32)


def paired_scan(decay, state, state_grad, axis, rider_fn, rider_inputs):
    peers = lax.axis_size(axis)
    if peers % 2:
        found = scanned_in([(decay, state, False), (decay, state_grad, True)], axis)
        return found[0], found[1], rider_fn(*rider_inputs)
    is_odd = lax.axis_index(axis) % 2 == 1
    swap = [(i, i ^ 1) for i in range(peers)]
    sent = jnp.where(is_odd, state_grad, state)
    message = packed(decay, sent, jnp.float32)
    if peers == 2:
        message, rider_inputs = lax.optimization_barrier((message, rider_inputs))
        riders = rider_fn(*rider_inputs)
    mate = lax.ppermute(message, axis, swap)
    if peers == 2:
        mate, riders = lax.optimization_barrier((mate, riders))
    mate_a, mate_s = unpacked(mate)
    own = jnp.where(is_odd, state, state_grad)
    window = (decay * mate_a, own + decay[:, None, None] * mate_s)
    near = (jnp.ones_like(decay), jnp.zeros_like(own))
    distance = 2
    while distance < peers:
        route = [(i, i + distance) for i in range(1, peers, 2) if i + distance < peers]
        route += [(i, i - distance) for i in range(0, peers, 2) if i - distance >= 0]
        if 2 * distance >= peers:
            far_s = lax.ppermute(window[1].astype(jnp.bfloat16), axis, route)
            if distance == 2:
                far_s, rider_inputs = lax.optimization_barrier((far_s, rider_inputs))
                riders = rider_fn(*rider_inputs)
            near = (near[0], near[1] + near[0][:, None, None] * far_s.astype(jnp.float32))
        else:
            far = lax.ppermute(packed(*window, jnp.bfloat16), axis, route)
            if distance == 2:
                far, rider_inputs = lax.optimization_barrier((far, rider_inputs))
                riders = rider_fn(*rider_inputs)
            far_a, far_s = unpacked(far)
            near = (near[0] * far_a, near[1] + near[0][:, None, None] * far_s)
            window = (window[0] * far_a, window[1] + window[0][:, None, None] * far_s)
        distance *= 2
    passing, riders = lax.optimization_barrier((near[1], riders))
    handed = lax.ppermute(passing, axis, swap)
    mine = mate_s + mate_a[:, None, None] * near[1]
    return jnp.where(is_odd, mine, handed), jnp.where(is_odd, handed, mine), riders


def shifted(block, axis, distance):
    devices = range(lax.axis_size(axis))
    route = [(i - distance, i) for i in devices if i - distance in devices]
    return lax.ppermute(block, axis, route)


def product(left, right):
    return jnp.dot(left, right, preferred_element_type=jnp.float32, precision=precise)


def body(
    conv_output, output_grad, write_keys, read_queries, log_decay, step_size, skip_gain, conv_weight
):
    length = conv_output.shape[0]
    head_count = log_decay.shape[1]
    head_width = conv_output.shape[1] // head_count
    parity = lax.axis_index("head") % 2
    own_first = parity == 0
    half = write_keys.shape[1]
    both = swapped(jnp.concatenate([write_keys, read_queries], 1), "head", 0)
    partner = (both[:, :half], both[:, half:])
    keys_full = jnp.where(
        own_first,
        jnp.concatenate([write_keys, partner[0]], 1),
        jnp.concatenate([partner[0], write_keys], 1),
    ).astype(jnp.float32)
    queries_full = jnp.where(
        own_first,
        jnp.concatenate([read_queries, partner[1]], 1),
        jnp.concatenate([partner[1], read_queries], 1),
    ).astype(jnp.float32)
    state_count = keys_full.shape[1]
    preact = conv_output.astype(jnp.float32)
    values = jax.nn.silu(preact)
    upstream = output_grad.astype(jnp.float32)
    values3 = values.reshape(length, head_count, head_width)
    upstream3 = upstream.reshape(length, head_count, head_width)
    cumulative = jnp.cumsum(log_decay, axis=0)
    totals = cumulative[-1]
    to_end = jnp.exp(totals[None, :] - cumulative)
    from_start = jnp.exp(cumulative)
    weighted = values3 * (to_end * step_size)[:, :, None]
    seeded = upstream3 * from_start[:, :, None]
    local_state = jnp.einsum("ln,lhp->hnp", keys_full, weighted, precision=precise)
    local_grad = jnp.einsum("ln,lhp->hnp", queries_full, seeded, precision=precise)
    decay_total = jnp.exp(totals)
    def local_terms(keys_full, queries_full, values3, upstream3, cumulative, step_size, preact):
        scores = product(queries_full, keys_full.T)
        row_ids = lax.broadcasted_iota(jnp.int32, (length, length), 0)
        col_ids = lax.broadcasted_iota(jnp.int32, (length, length), 1)
        causal = row_ids >= col_ids
        cum_heads = cumulative.T
        step_heads = step_size.T
        log_gap = jnp.where(causal[None], cum_heads[:, :, None] - cum_heads[:, None, :], -1e30)
        decay_mask = jnp.exp(log_gap)
        pair_dots = jnp.einsum("thp,shp->hts", upstream3, values3, precision=precise)
        masked_scores = decay_mask * scores[None]
        weight_sum = jnp.einsum("hts,hs->ts", decay_mask * pair_dots, step_heads, precision=precise)
        within = jnp.einsum(
            "hts,thp->shp", masked_scores * step_heads[:, None, :], upstream3, precision=precise
        )
        effect = masked_scores * pair_dots
        row_sums = jnp.einsum("hts,hs->th", effect, step_heads, precision=precise)
        col_sums = jnp.sum(effect, 1).T
        logistic = jax.nn.sigmoid(preact)
        return (
            within + skip_gain[None, :, None] * upstream3,
            row_sums - col_sums * step_size,
            col_sums,
            product(weight_sum, keys_full),
            lax.dot_general(
                weight_sum,
                queries_full,
                (((0,), (0,)), ((), ())),
                preferred_element_type=jnp.float32,
                precision=precise,
            ),
            logistic * (1.0 + preact * (1.0 - logistic)),
        )
    def local_block(*inputs):
        always = lax.axis_index("seq") >= 0
        return lax.cond(
            always,
            local_terms,
            lambda *a: jax.tree.map(jnp.zeros_like, local_terms(*a)),
            *inputs,
        )

    entering, arriving, riders = paired_scan(
        decay_total,
        local_state,
        local_grad,
        "seq",
        local_block,
        (keys_full, queries_full, values3, upstream3, cumulative, step_size, preact),
    )
    within_part, local_decay, col_sums, query_local, key_local, silu_slope = riders
    from_state = jnp.einsum("ln,hnp->lhp", queries_full, entering, precision=precise)
    into_state = jnp.einsum("ln,hnp->lhp", keys_full, arriving, precision=precise)
    carried = jnp.sum(values3 * into_state, 2)
    step_grad = col_sums + to_end * carried
    value_grad = within_part + (to_end * step_size)[:, :, None] * into_state
    leaving = decay_total[:, None, None] * entering + local_state
    decay_terms = (
        local_decay
        + from_start * jnp.sum(upstream3 * from_state, 2)
        - to_end * step_size * carried
    )
    last_row = (lax.broadcasted_iota(jnp.int32, (length, 1), 0) == length - 1).astype(jnp.float32)
    decay_terms = decay_terms + last_row * jnp.sum(arriving * leaving, (1, 2))[None, :]
    decay_grad = jnp.flip(jnp.cumsum(jnp.flip(decay_terms, 0), 0), 0)
    query_part = query_local + jnp.einsum(
        "lhp,hnp->ln", seeded, entering, precision=precise
    )
    key_part = key_local + jnp.einsum("lhp,hnp->ln", weighted, arriving, precision=precise)
    half_width = state_count // 2
    key_mine = jnp.where(own_first, key_part[:, :half_width], key_part[:, half_width:])
    key_other = jnp.where(own_first, key_part[:, half_width:], key_part[:, :half_width])
    query_mine = jnp.where(own_first, query_part[:, :half_width], query_part[:, half_width:])
    query_other = jnp.where(own_first, query_part[:, half_width:], query_part[:, :half_width])
    sent_back = swapped(
        jnp.concatenate([key_other, query_other], 1).astype(jnp.bfloat16), "head", 0
    ).astype(key_other.dtype)
    received = (sent_back[:, :half_width], sent_back[:, half_width:])
    keys_grad = key_mine + received[0]
    queries_grad = query_mine + received[1]
    conv_grad = value_grad.reshape(length, -1) * silu_slope
    following = shifted(conv_grad[:3], "seq", -1)
    extended = jnp.concatenate([conv_grad, following], 0)
    input_grad = jnp.zeros_like(conv_grad)
    for offset in range(4):
        input_grad = (
            input_grad + conv_weight[offset][None, :] * extended[3 - offset : 3 - offset + length]
        )
    return (input_grad.astype(jnp.bfloat16), keys_grad, queries_grad, decay_grad, step_grad)


def solution(mesh):
    return jax.shard_map(
        body,
        mesh=mesh,
        in_specs=(
            P("seq", "head"),
            P("seq", "head"),
            P("seq", "head"),
            P("seq", "head"),
            P("seq", "head"),
            P("seq", "head"),
            P("head"),
            P(None, "head"),
        ),
        out_specs=(
            P("seq", "head"),
            P("seq", "head"),
            P("seq", "head"),
            P("seq", "head"),
            P("seq", "head"),
        ),
        check_vma=False,
    )
```

```python
import jax
import jax.numpy as jnp
from jax import lax
from jax.sharding import PartitionSpec as P

precise = lax.Precision.HIGHEST
split_bf16 = lax.Precision.HIGH


def swapped(block, axis, bit):
    count = lax.axis_size(axis)
    route = []
    for low in range(count):
        high = low | 1 << bit
        if high != low and high < count:
            route += [(low, high), (high, low)]
    return lax.ppermute(block, axis, route)


def scanned_in(shards, axis):
    peers = lax.axis_size(axis)
    near = [(jnp.ones_like(a), jnp.zeros_like(s)) for a, s, _ in shards]
    window = [(a, s) for a, s, _ in shards]
    distance = 1
    while distance < peers:
        routes = []
        for _, _, reverse in shards:
            step = -distance if reverse else distance
            routes.append([(i, i + step) for i in range(peers) if 0 <= i + step < peers])
        received = [lax.ppermute(w, axis, r) for w, r in zip(window, routes)]
        more = 2 * distance < peers
        for k, (far_a, far_s) in enumerate(received):
            near_a, near_s = near[k]
            near[k] = (near_a * far_a, near_s + near_a[:, None, None] * far_s)
            if more:
                win_a, win_s = window[k]
                window[k] = (win_a * far_a, win_s + win_a[:, None, None] * far_s)
        distance *= 2
    return [s for _, s in near]


def packed(decay, state, kind):
    heads, width = state.shape[0], state.shape[1]
    if kind == jnp.float32:
        parts = decay
    else:
        high = decay.astype(kind)
        parts = jnp.concatenate([high, (decay - high.astype(decay.dtype)).astype(kind)])
    row = jnp.pad(parts.astype(kind), (0, width - parts.shape[0]))
    slab = jnp.broadcast_to(row[None, :, None], (1,) + state.shape[1:])
    return jnp.concatenate([state.astype(kind), slab], 0)


def unpacked(message):
    heads = message.shape[0] - 1
    row = message[heads, :, 0].astype(jnp.float32)
    decay = row[:heads] if message.dtype == jnp.float32 else row[:heads] + row[heads : 2 * heads]
    return decay, message[:heads].astype(jnp.float32)


def paired_scan(decay, state, state_grad, axis, rider_fn, rider_inputs):
    peers = lax.axis_size(axis)
    if peers % 2:
        found = scanned_in([(decay, state, False), (decay, state_grad, True)], axis)
        return found[0], found[1], rider_fn(*rider_inputs)
    is_odd = lax.axis_index(axis) % 2 == 1
    swap = [(i, i ^ 1) for i in range(peers)]
    sent = jnp.where(is_odd, state_grad, state)
    message = packed(decay, sent, jnp.float32)
    if peers == 2:
        message, rider_inputs = lax.optimization_barrier((message, rider_inputs))
        riders = rider_fn(*rider_inputs)
    mate = lax.ppermute(message, axis, swap)
    if peers == 2:
        mate, riders = lax.optimization_barrier((mate, riders))
    mate_a, mate_s = unpacked(mate)
    own = jnp.where(is_odd, state, state_grad)
    window = (decay * mate_a, own + decay[:, None, None] * mate_s)
    near = (jnp.ones_like(decay), jnp.zeros_like(own))
    distance = 2
    while distance < peers:
        route = [(i, i + distance) for i in range(1, peers, 2) if i + distance < peers]
        route += [(i, i - distance) for i in range(0, peers, 2) if i - distance >= 0]
        if 2 * distance >= peers:
            far_s = lax.ppermute(window[1].astype(jnp.bfloat16), axis, route)
            if distance == 2:
                far_s, rider_inputs = lax.optimization_barrier((far_s, rider_inputs))
                riders = rider_fn(*rider_inputs)
            near = (near[0], near[1] + near[0][:, None, None] * far_s.astype(jnp.float32))
        else:
            far = lax.ppermute(packed(*window, jnp.bfloat16), axis, route)
            if distance == 2:
                far, rider_inputs = lax.optimization_barrier((far, rider_inputs))
                riders = rider_fn(*rider_inputs)
            far_a, far_s = unpacked(far)
            near = (near[0] * far_a, near[1] + near[0][:, None, None] * far_s)
            window = (window[0] * far_a, window[1] + window[0][:, None, None] * far_s)
        distance *= 2
    passing, riders = lax.optimization_barrier((near[1], riders))
    handed = lax.ppermute(passing, axis, swap)
    mine = mate_s + mate_a[:, None, None] * near[1]
    return jnp.where(is_odd, mine, handed), jnp.where(is_odd, handed, mine), riders


def shifted(block, axis, distance):
    devices = range(lax.axis_size(axis))
    route = [(i - distance, i) for i in devices if i - distance in devices]
    return lax.ppermute(block, axis, route)


def product(left, right):
    return jnp.dot(left, right, preferred_element_type=jnp.float32, precision=precise)


def body(
    conv_output, output_grad, write_keys, read_queries, log_decay, step_size, skip_gain, conv_weight
):
    length = conv_output.shape[0]
    head_count = log_decay.shape[1]
    head_width = conv_output.shape[1] // head_count
    parity = lax.axis_index("head") % 2
    own_first = parity == 0
    half = write_keys.shape[1]
    both = swapped(jnp.concatenate([write_keys, read_queries], 1), "head", 0)
    partner = (both[:, :half], both[:, half:])
    keys_full = jnp.where(
        own_first,
        jnp.concatenate([write_keys, partner[0]], 1),
        jnp.concatenate([partner[0], write_keys], 1),
    ).astype(jnp.float32)
    queries_full = jnp.where(
        own_first,
        jnp.concatenate([read_queries, partner[1]], 1),
        jnp.concatenate([partner[1], read_queries], 1),
    ).astype(jnp.float32)
    state_count = keys_full.shape[1]
    preact = conv_output.astype(jnp.float32)
    values = jax.nn.silu(preact)
    upstream = output_grad.astype(jnp.float32)
    values3 = values.reshape(length, head_count, head_width)
    upstream3 = upstream.reshape(length, head_count, head_width)
    cumulative = jnp.cumsum(log_decay, axis=0)
    totals = cumulative[-1]
    to_end = jnp.exp(totals[None, :] - cumulative)
    from_start = jnp.exp(cumulative)
    weighted = values3 * (to_end * step_size)[:, :, None]
    seeded = upstream3 * from_start[:, :, None]
    local_state = jnp.einsum("ln,lhp->hnp", keys_full, weighted, precision=split_bf16)
    local_grad = jnp.einsum("ln,lhp->hnp", queries_full, seeded, precision=split_bf16)
    decay_total = jnp.exp(totals)
    def local_terms(keys_full, queries_full, values3, upstream3, cumulative, step_size, preact):
        scores = product(queries_full, keys_full.T)
        row_ids = lax.broadcasted_iota(jnp.int32, (length, length), 0)
        col_ids = lax.broadcasted_iota(jnp.int32, (length, length), 1)
        causal = row_ids >= col_ids
        cum_heads = cumulative.T
        step_heads = step_size.T
        log_gap = jnp.where(causal[None], cum_heads[:, :, None] - cum_heads[:, None, :], -1e30)
        decay_mask = jnp.exp(log_gap)
        pair_dots = jnp.einsum("thp,shp->hts", upstream3, values3, precision=precise)
        masked_scores = decay_mask * scores[None]
        weight_sum = jnp.einsum("hts,hs->ts", decay_mask * pair_dots, step_heads, precision=precise)
        within = jnp.einsum(
            "hts,thp->shp", masked_scores * step_heads[:, None, :], upstream3, precision=precise
        )
        effect = masked_scores * pair_dots
        row_sums = jnp.einsum("hts,hs->th", effect, step_heads, precision=precise)
        col_sums = jnp.sum(effect, 1).T
        logistic = jax.nn.sigmoid(preact)
        return (
            within + skip_gain[None, :, None] * upstream3,
            row_sums - col_sums * step_size,
            col_sums,
            product(weight_sum, keys_full),
            lax.dot_general(
                weight_sum,
                queries_full,
                (((0,), (0,)), ((), ())),
                preferred_element_type=jnp.float32,
                precision=precise,
            ),
            logistic * (1.0 + preact * (1.0 - logistic)),
        )
    def local_block(*inputs):
        always = lax.axis_index("seq") >= 0
        return lax.cond(
            always,
            local_terms,
            lambda *a: jax.tree.map(jnp.zeros_like, local_terms(*a)),
            *inputs,
        )

    entering, arriving, riders = paired_scan(
        decay_total,
        local_state,
        local_grad,
        "seq",
        local_block,
        (keys_full, queries_full, values3, upstream3, cumulative, step_size, preact),
    )
    within_part, local_decay, col_sums, query_local, key_local, silu_slope = riders
    from_state = jnp.einsum("ln,hnp->lhp", queries_full, entering, precision=split_bf16)
    into_state = jnp.einsum("ln,hnp->lhp", keys_full, arriving, precision=split_bf16)
    carried = jnp.sum(values3 * into_state, 2)
    step_grad = col_sums + to_end * carried
    value_grad = within_part + (to_end * step_size)[:, :, None] * into_state
    leaving = decay_total[:, None, None] * entering + local_state
    decay_terms = (
        local_decay
        + from_start * jnp.sum(upstream3 * from_state, 2)
        - to_end * step_size * carried
    )
    last_row = (lax.broadcasted_iota(jnp.int32, (length, 1), 0) == length - 1).astype(jnp.float32)
    decay_terms = decay_terms + last_row * jnp.sum(arriving * leaving, (1, 2))[None, :]
    decay_grad = jnp.flip(jnp.cumsum(jnp.flip(decay_terms, 0), 0), 0)
    half_width = state_count // 2
    other_at = jnp.where(own_first, half_width, 0)
    mine_at = half_width - other_at

    def key_query_half(at):
        pick = lambda part: lax.dynamic_slice_in_dim(part, at, half_width, 1)
        return (
            pick(key_local)
            + jnp.einsum("lhp,hnp->ln", weighted, pick(arriving), precision=precise),
            pick(query_local)
            + jnp.einsum("lhp,hnp->ln", seeded, pick(entering), precision=precise),
        )

    key_other, query_other = key_query_half(other_at)
    sent_back = swapped(
        jnp.concatenate([key_other, query_other], 1).astype(jnp.bfloat16), "head", 0
    ).astype(key_other.dtype)
    key_mine, query_mine = key_query_half(mine_at)
    keys_grad = key_mine + sent_back[:, :half_width]
    queries_grad = query_mine + sent_back[:, half_width:]
    head_rows = within_part[:3] + (to_end * step_size)[:3, :, None] * jnp.einsum(
        "ln,hnp->lhp", keys_full[:3], arriving, precision=split_bf16
    )
    following = shifted(head_rows.reshape(3, -1) * silu_slope[:3], "seq", -1)
    conv_grad = value_grad.reshape(length, -1) * silu_slope
    extended = jnp.concatenate([conv_grad, following], 0)
    input_grad = jnp.zeros_like(conv_grad)
    for offset in range(4):
        input_grad = (
            input_grad + conv_weight[offset][None, :] * extended[3 - offset : 3 - offset + length]
        )
    return (input_grad.astype(jnp.bfloat16), keys_grad, queries_grad, decay_grad, step_grad)


def solution(mesh):
    return jax.shard_map(
        body,
        mesh=mesh,
        in_specs=(
            P("seq", "head"),
            P("seq", "head"),
            P("seq", "head"),
            P("seq", "head"),
            P("seq", "head"),
            P("seq", "head"),
            P("head"),
            P(None, "head"),
        ),
        out_specs=(
            P("seq", "head"),
            P("seq", "head"),
            P("seq", "head"),
            P("seq", "head"),
            P("seq", "head"),
        ),
        check_vma=False,
    )
```

```python
import jax
import jax.numpy as jnp
from jax import lax
from jax.sharding import PartitionSpec as P

precise = lax.Precision.HIGHEST
split_bf16 = lax.Precision.HIGH


def swapped(block, axis, bit):
    count = lax.axis_size(axis)
    route = []
    for low in range(count):
        high = low | 1 << bit
        if high != low and high < count:
            route += [(low, high), (high, low)]
    return lax.ppermute(block, axis, route)


def scanned_in(shards, axis):
    peers = lax.axis_size(axis)
    near = [(jnp.ones_like(a), jnp.zeros_like(s)) for a, s, _ in shards]
    window = [(a, s) for a, s, _ in shards]
    distance = 1
    while distance < peers:
        routes = []
        for _, _, reverse in shards:
            step = -distance if reverse else distance
            routes.append([(i, i + step) for i in range(peers) if 0 <= i + step < peers])
        received = [lax.ppermute(w, axis, r) for w, r in zip(window, routes)]
        more = 2 * distance < peers
        for k, (far_a, far_s) in enumerate(received):
            near_a, near_s = near[k]
            near[k] = (near_a * far_a, near_s + near_a[:, None, None] * far_s)
            if more:
                win_a, win_s = window[k]
                window[k] = (win_a * far_a, win_s + win_a[:, None, None] * far_s)
        distance *= 2
    return [s for _, s in near]


def packed(decay, state, kind):
    heads, width = state.shape[0], state.shape[1]
    if kind == jnp.float32:
        parts = decay
    else:
        high = decay.astype(kind)
        parts = jnp.concatenate([high, (decay - high.astype(decay.dtype)).astype(kind)])
    row = jnp.pad(parts.astype(kind), (0, width - parts.shape[0]))
    slab = jnp.broadcast_to(row[None, :, None], (1,) + state.shape[1:])
    return jnp.concatenate([state.astype(kind), slab], 0)


def unpacked(message):
    heads = message.shape[0] - 1
    row = message[heads, :, 0].astype(jnp.float32)
    decay = row[:heads] if message.dtype == jnp.float32 else row[:heads] + row[heads : 2 * heads]
    return decay, message[:heads].astype(jnp.float32)


def paired_scan(decay, state, state_grad, axis, rider_fn, rider_inputs):
    peers = lax.axis_size(axis)
    if peers % 2:
        found = scanned_in([(decay, state, False), (decay, state_grad, True)], axis)
        return found[0], found[1], rider_fn(*rider_inputs)
    is_odd = lax.axis_index(axis) % 2 == 1
    swap = [(i, i ^ 1) for i in range(peers)]
    sent = jnp.where(is_odd, state_grad, state)
    message = packed(decay, sent, jnp.float32)
    if peers == 2:
        message, rider_inputs = lax.optimization_barrier((message, rider_inputs))
        riders = rider_fn(*rider_inputs)
    mate = lax.ppermute(message, axis, swap)
    if peers == 2:
        mate, riders = lax.optimization_barrier((mate, riders))
    mate_a, mate_s = unpacked(mate)
    own = jnp.where(is_odd, state, state_grad)
    window = (decay * mate_a, own + decay[:, None, None] * mate_s)
    near = (jnp.ones_like(decay), jnp.zeros_like(own))
    distance = 2
    while distance < peers:
        route = [(i, i + distance) for i in range(1, peers, 2) if i + distance < peers]
        route += [(i, i - distance) for i in range(0, peers, 2) if i - distance >= 0]
        if 2 * distance >= peers:
            far_s = lax.ppermute(window[1].astype(jnp.bfloat16), axis, route)
            if distance == 2:
                far_s, rider_inputs = lax.optimization_barrier((far_s, rider_inputs))
                riders = rider_fn(*rider_inputs)
            near = (near[0], near[1] + near[0][:, None, None] * far_s.astype(jnp.float32))
        else:
            far = lax.ppermute(packed(*window, jnp.bfloat16), axis, route)
            if distance == 2:
                far, rider_inputs = lax.optimization_barrier((far, rider_inputs))
                riders = rider_fn(*rider_inputs)
            far_a, far_s = unpacked(far)
            near = (near[0] * far_a, near[1] + near[0][:, None, None] * far_s)
            window = (window[0] * far_a, window[1] + window[0][:, None, None] * far_s)
        distance *= 2
    passing, riders = lax.optimization_barrier((near[1], riders))
    handed = lax.ppermute(passing, axis, swap)
    mine = mate_s + mate_a[:, None, None] * near[1]
    return jnp.where(is_odd, mine, handed), jnp.where(is_odd, handed, mine), riders


def shifted(block, axis, distance):
    devices = range(lax.axis_size(axis))
    route = [(i - distance, i) for i in devices if i - distance in devices]
    return lax.ppermute(block, axis, route)


def product(left, right):
    return jnp.dot(left, right, preferred_element_type=jnp.float32, precision=precise)


def body(
    conv_output, output_grad, write_keys, read_queries, log_decay, step_size, skip_gain, conv_weight
):
    length = conv_output.shape[0]
    head_count = log_decay.shape[1]
    head_width = conv_output.shape[1] // head_count
    parity = lax.axis_index("head") % 2
    own_first = parity == 0
    half = write_keys.shape[1]
    partner = swapped((write_keys, read_queries), "head", 0)
    keys_full = jnp.where(
        own_first,
        jnp.concatenate([write_keys, partner[0]], 1),
        jnp.concatenate([partner[0], write_keys], 1),
    ).astype(jnp.float32)
    queries_full = jnp.where(
        own_first,
        jnp.concatenate([read_queries, partner[1]], 1),
        jnp.concatenate([partner[1], read_queries], 1),
    ).astype(jnp.float32)
    state_count = keys_full.shape[1]
    preact = conv_output.astype(jnp.float32)
    values = jax.nn.silu(preact)
    upstream = output_grad.astype(jnp.float32)
    values3 = values.reshape(length, head_count, head_width)
    upstream3 = upstream.reshape(length, head_count, head_width)
    cumulative = jnp.cumsum(log_decay, axis=0)
    totals = cumulative[-1]
    to_end = jnp.exp(totals[None, :] - cumulative)
    from_start = jnp.exp(cumulative)
    weighted = values3 * (to_end * step_size)[:, :, None]
    seeded = upstream3 * from_start[:, :, None]
    local_state = jnp.einsum("ln,lhp->hnp", keys_full, weighted, precision=split_bf16)
    local_grad = jnp.einsum("ln,lhp->hnp", queries_full, seeded, precision=split_bf16)
    decay_total = jnp.exp(totals)
    def local_terms(keys_full, queries_full, values3, upstream3, cumulative, step_size, preact):
        scores = product(queries_full, keys_full.T)
        row_ids = lax.broadcasted_iota(jnp.int32, (length, length), 0)
        col_ids = lax.broadcasted_iota(jnp.int32, (length, length), 1)
        causal = row_ids >= col_ids
        cum_heads = cumulative.T
        step_heads = step_size.T
        log_gap = jnp.where(causal[None], cum_heads[:, :, None] - cum_heads[:, None, :], -1e30)
        decay_mask = jnp.exp(log_gap)
        pair_dots = jnp.einsum("thp,shp->hts", upstream3, values3, precision=precise)
        masked_scores = decay_mask * scores[None]
        weight_sum = jnp.einsum("hts,hs->ts", decay_mask * pair_dots, step_heads, precision=precise)
        within = jnp.einsum(
            "hts,thp->shp", masked_scores * step_heads[:, None, :], upstream3, precision=precise
        )
        effect = masked_scores * pair_dots
        row_sums = jnp.einsum("hts,hs->th", effect, step_heads, precision=precise)
        col_sums = jnp.sum(effect, 1).T
        logistic = jax.nn.sigmoid(preact)
        return (
            within + skip_gain[None, :, None] * upstream3,
            row_sums - col_sums * step_size,
            col_sums,
            product(weight_sum, keys_full),
            lax.dot_general(
                weight_sum,
                queries_full,
                (((0,), (0,)), ((), ())),
                preferred_element_type=jnp.float32,
                precision=precise,
            ),
            logistic * (1.0 + preact * (1.0 - logistic)),
        )
    def local_block(*inputs):
        always = lax.axis_index("seq") >= 0
        return lax.cond(
            always,
            local_terms,
            lambda *a: jax.tree.map(jnp.zeros_like, local_terms(*a)),
            *inputs,
        )

    entering, arriving, riders = paired_scan(
        decay_total,
        local_state,
        local_grad,
        "seq",
        local_block,
        (keys_full, queries_full, values3, upstream3, cumulative, step_size, preact),
    )
    within_part, local_decay, col_sums, query_local, key_local, silu_slope = riders
    from_state = jnp.einsum("ln,hnp->lhp", queries_full, entering, precision=precise)
    into_state = jnp.einsum("ln,hnp->lhp", keys_full, arriving, precision=precise)
    carried = jnp.sum(values3 * into_state, 2)
    step_grad = col_sums + to_end * carried
    value_grad = within_part + (to_end * step_size)[:, :, None] * into_state
    leaving = decay_total[:, None, None] * entering + local_state
    decay_terms = (
        local_decay
        + from_start * jnp.sum(upstream3 * from_state, 2)
        - to_end * step_size * carried
    )
    last_row = (lax.broadcasted_iota(jnp.int32, (length, 1), 0) == length - 1).astype(jnp.float32)
    decay_terms = decay_terms + last_row * jnp.sum(arriving * leaving, (1, 2))[None, :]
    decay_grad = jnp.flip(jnp.cumsum(jnp.flip(decay_terms, 0), 0), 0)
    query_part = query_local + jnp.einsum(
        "lhp,hnp->ln", seeded, entering, precision=precise
    )
    key_part = key_local + jnp.einsum("lhp,hnp->ln", weighted, arriving, precision=precise)
    half_width = state_count // 2
    key_mine = jnp.where(own_first, key_part[:, :half_width], key_part[:, half_width:])
    key_other = jnp.where(own_first, key_part[:, half_width:], key_part[:, :half_width])
    query_mine = jnp.where(own_first, query_part[:, :half_width], query_part[:, half_width:])
    query_other = jnp.where(own_first, query_part[:, half_width:], query_part[:, :half_width])
    sent_back = swapped(
        jnp.concatenate([key_other, query_other], 1).astype(jnp.bfloat16), "head", 0
    ).astype(key_other.dtype)
    received = (sent_back[:, :half_width], sent_back[:, half_width:])
    keys_grad = key_mine + received[0]
    queries_grad = query_mine + received[1]
    conv_grad = value_grad.reshape(length, -1) * silu_slope
    following = shifted(conv_grad[:3], "seq", -1)
    extended = jnp.concatenate([conv_grad, following], 0)
    input_grad = jnp.zeros_like(conv_grad)
    for offset in range(4):
        input_grad = (
            input_grad + conv_weight[offset][None, :] * extended[3 - offset : 3 - offset + length]
        )
    return (input_grad.astype(jnp.bfloat16), keys_grad, queries_grad, decay_grad, step_grad)


def solution(mesh):
    return jax.shard_map(
        body,
        mesh=mesh,
        in_specs=(
            P("seq", "head"),
            P("seq", "head"),
            P("seq", "head"),
            P("seq", "head"),
            P("seq", "head"),
            P("seq", "head"),
            P("head"),
            P(None, "head"),
        ),
        out_specs=(
            P("seq", "head"),
            P("seq", "head"),
            P("seq", "head"),
            P("seq", "head"),
            P("seq", "head"),
        ),
        check_vma=False,
    )
```

```python
import jax
import jax.numpy as jnp
from jax import lax
from jax.sharding import PartitionSpec as P

precise = lax.Precision.HIGHEST


def swapped(block, axis, bit):
    count = lax.axis_size(axis)
    route = []
    for low in range(count):
        high = low | 1 << bit
        if high != low and high < count:
            route += [(low, high), (high, low)]
    return lax.ppermute(block, axis, route)


def scanned_in(shards, axis):
    peers = lax.axis_size(axis)
    near = [(jnp.ones_like(a), jnp.zeros_like(s)) for a, s, _ in shards]
    window = [(a, s) for a, s, _ in shards]
    distance = 1
    while distance < peers:
        routes = []
        for _, _, reverse in shards:
            step = -distance if reverse else distance
            routes.append([(i, i + step) for i in range(peers) if 0 <= i + step < peers])
        received = [lax.ppermute(w, axis, r) for w, r in zip(window, routes)]
        more = 2 * distance < peers
        for k, (far_a, far_s) in enumerate(received):
            near_a, near_s = near[k]
            near[k] = (near_a * far_a, near_s + near_a[:, None, None] * far_s)
            if more:
                win_a, win_s = window[k]
                window[k] = (win_a * far_a, win_s + win_a[:, None, None] * far_s)
        distance *= 2
    return [s for _, s in near]


def packed(decay, state, kind):
    heads, width = state.shape[0], state.shape[1]
    if kind == jnp.float32:
        parts = decay
    else:
        high = decay.astype(kind)
        parts = jnp.concatenate([high, (decay - high.astype(decay.dtype)).astype(kind)])
    row = jnp.pad(parts.astype(kind), (0, width - parts.shape[0]))
    slab = jnp.broadcast_to(row[None, :, None], (1,) + state.shape[1:])
    return jnp.concatenate([state.astype(kind), slab], 0)


def unpacked(message):
    heads = message.shape[0] - 1
    row = message[heads, :, 0].astype(jnp.float32)
    decay = row[:heads] if message.dtype == jnp.float32 else row[:heads] + row[heads : 2 * heads]
    return decay, message[:heads].astype(jnp.float32)


def paired_scan(decay, state, state_grad, axis, rider_fn, rider_inputs):
    peers = lax.axis_size(axis)
    if peers % 2:
        found = scanned_in([(decay, state, False), (decay, state_grad, True)], axis)
        return found[0], found[1], rider_fn(*rider_inputs)
    is_odd = lax.axis_index(axis) % 2 == 1
    swap = [(i, i ^ 1) for i in range(peers)]
    sent = jnp.where(is_odd, state_grad, state)
    message = packed(decay, sent, jnp.float32)
    if peers == 2:
        message, rider_inputs = lax.optimization_barrier((message, rider_inputs))
        riders = rider_fn(*rider_inputs)
    mate = lax.ppermute(message, axis, swap)
    if peers == 2:
        mate, riders = lax.optimization_barrier((mate, riders))
    mate_a, mate_s = unpacked(mate)
    own = jnp.where(is_odd, state, state_grad)
    window = (decay * mate_a, own + decay[:, None, None] * mate_s)
    near = (jnp.ones_like(decay), jnp.zeros_like(own))
    distance = 2
    while distance < peers:
        route = [(i, i + distance) for i in range(1, peers, 2) if i + distance < peers]
        route += [(i, i - distance) for i in range(0, peers, 2) if i - distance >= 0]
        if 2 * distance >= peers:
            far_s = lax.ppermute(window[1].astype(jnp.bfloat16), axis, route)
            if distance == 2:
                far_s, rider_inputs = lax.optimization_barrier((far_s, rider_inputs))
                riders = rider_fn(*rider_inputs)
            near = (near[0], near[1] + near[0][:, None, None] * far_s.astype(jnp.float32))
        else:
            far = lax.ppermute(packed(*window, jnp.bfloat16), axis, route)
            if distance == 2:
                far, rider_inputs = lax.optimization_barrier((far, rider_inputs))
                riders = rider_fn(*rider_inputs)
            far_a, far_s = unpacked(far)
            near = (near[0] * far_a, near[1] + near[0][:, None, None] * far_s)
            window = (window[0] * far_a, window[1] + window[0][:, None, None] * far_s)
        distance *= 2
    passing, riders = lax.optimization_barrier((near[1], riders))
    handed = lax.ppermute(passing, axis, swap)
    mine = mate_s + mate_a[:, None, None] * near[1]
    return jnp.where(is_odd, mine, handed), jnp.where(is_odd, handed, mine), riders


def shifted(block, axis, distance):
    devices = range(lax.axis_size(axis))
    route = [(i - distance, i) for i in devices if i - distance in devices]
    return lax.ppermute(block, axis, route)


def product(left, right):
    return jnp.dot(left, right, preferred_element_type=jnp.float32, precision=precise)


def body(
    conv_output, output_grad, write_keys, read_queries, log_decay, step_size, skip_gain, conv_weight
):
    length = conv_output.shape[0]
    head_count = log_decay.shape[1]
    head_width = conv_output.shape[1] // head_count
    parity = lax.axis_index("head") % 2
    own_first = parity == 0
    half = write_keys.shape[1]
    both = swapped(jnp.concatenate([write_keys, read_queries], 1), "head", 0)
    partner = (both[:, :half], both[:, half:])
    keys_full = jnp.where(
        own_first,
        jnp.concatenate([write_keys, partner[0]], 1),
        jnp.concatenate([partner[0], write_keys], 1),
    ).astype(jnp.float32)
    queries_full = jnp.where(
        own_first,
        jnp.concatenate([read_queries, partner[1]], 1),
        jnp.concatenate([partner[1], read_queries], 1),
    ).astype(jnp.float32)
    state_count = keys_full.shape[1]
    preact = conv_output.astype(jnp.float32)
    values = jax.nn.silu(preact)
    upstream = output_grad.astype(jnp.float32)
    values3 = values.reshape(length, head_count, head_width)
    upstream3 = upstream.reshape(length, head_count, head_width)
    cumulative = jnp.cumsum(log_decay, axis=0)
    totals = cumulative[-1]
    to_end = jnp.exp(totals[None, :] - cumulative)
    from_start = jnp.exp(cumulative)
    weighted = values3 * (to_end * step_size)[:, :, None]
    seeded = upstream3 * from_start[:, :, None]
    local_state = jnp.einsum("ln,lhp->hnp", keys_full, weighted, precision=precise)
    local_grad = jnp.einsum("ln,lhp->hnp", queries_full, seeded, precision=precise)
    decay_total = jnp.exp(totals)
    def local_terms(keys_full, queries_full, values3, upstream3, cumulative, step_size, preact):
        scores = product(queries_full, keys_full.T)
        row_ids = lax.broadcasted_iota(jnp.int32, (length, length), 0)
        col_ids = lax.broadcasted_iota(jnp.int32, (length, length), 1)
        causal = row_ids >= col_ids
        cum_heads = cumulative.T
        step_heads = step_size.T
        log_gap = jnp.where(causal[None], cum_heads[:, :, None] - cum_heads[:, None, :], -1e30)
        decay_mask = jnp.exp(log_gap)
        pair_dots = jnp.einsum("thp,shp->hts", upstream3, values3, precision=precise)
        masked_scores = decay_mask * scores[None]
        weight_sum = jnp.einsum("hts,hs->ts", decay_mask * pair_dots, step_heads, precision=precise)
        within = jnp.einsum(
            "hts,thp->shp", masked_scores * step_heads[:, None, :], upstream3, precision=precise
        )
        effect = masked_scores * pair_dots
        row_sums = jnp.einsum("hts,hs->th", effect, step_heads, precision=precise)
        col_sums = jnp.sum(effect, 1).T
        logistic = jax.nn.sigmoid(preact)
        return (
            within + skip_gain[None, :, None] * upstream3,
            row_sums - col_sums * step_size,
            col_sums,
            product(weight_sum, keys_full),
            lax.dot_general(
                weight_sum,
                queries_full,
                (((0,), (0,)), ((), ())),
                preferred_element_type=jnp.float32,
                precision=precise,
            ),
            logistic * (1.0 + preact * (1.0 - logistic)),
        )
    def local_block(*inputs):
        always = lax.axis_index("seq") >= 0
        return lax.cond(
            always,
            local_terms,
            lambda *a: jax.tree.map(jnp.zeros_like, local_terms(*a)),
            *inputs,
        )

    entering, arriving, riders = paired_scan(
        decay_total,
        local_state,
        local_grad,
        "seq",
        local_block,
        (keys_full, queries_full, values3, upstream3, cumulative, step_size, preact),
    )
    within_part, local_decay, col_sums, query_local, key_local, silu_slope = riders
    half_width = state_count // 2
    other_at = jnp.where(own_first, half_width, 0)
    mine_at = half_width - other_at

    def key_query_half(at, arriving, entering):
        pick = lambda part: lax.dynamic_slice_in_dim(part, at, half_width, 1)
        return (
            pick(key_local)
            + jnp.einsum("lhp,hnp->ln", weighted, pick(arriving), precision=precise),
            pick(query_local)
            + jnp.einsum("lhp,hnp->ln", seeded, pick(entering), precision=precise),
        )

    key_other, query_other = key_query_half(other_at, arriving, entering)
    outgoing = jnp.concatenate([key_other, query_other], 1).astype(jnp.bfloat16)
    head_rows = within_part[:3] + (to_end * step_size)[:3, :, None] * jnp.einsum(
        "ln,hnp->lhp", keys_full[:3], arriving, precision=precise
    )
    head_rows = head_rows.reshape(3, -1) * silu_slope[:3]
    outgoing, head_rows, entering, arriving = lax.optimization_barrier(
        (outgoing, head_rows, entering, arriving)
    )
    sent_back = swapped(outgoing, "head", 0).astype(jnp.float32)
    following = shifted(head_rows, "seq", -1)

    def remaining(entering, arriving):
        from_state = jnp.einsum("ln,hnp->lhp", queries_full, entering, precision=precise)
        into_state = jnp.einsum("ln,hnp->lhp", keys_full, arriving, precision=precise)
        carried = jnp.sum(values3 * into_state, 2)
        step_grad = col_sums + to_end * carried
        value_grad = within_part + (to_end * step_size)[:, :, None] * into_state
        leaving = decay_total[:, None, None] * entering + local_state
        decay_terms = (
            local_decay
            + from_start * jnp.sum(upstream3 * from_state, 2)
            - to_end * step_size * carried
        )
        last_row = lax.broadcasted_iota(jnp.int32, (length, 1), 0) == length - 1
        decay_terms = decay_terms + last_row.astype(jnp.float32) * jnp.sum(
            arriving * leaving, (1, 2)
        )[None, :]
        decay_grad = jnp.flip(jnp.cumsum(jnp.flip(decay_terms, 0), 0), 0)
        key_mine, query_mine = key_query_half(mine_at, arriving, entering)
        conv_grad = value_grad.reshape(length, -1) * silu_slope
        return decay_grad, step_grad, key_mine, query_mine, conv_grad

    always = lax.axis_index("seq") >= 0
    rest = lax.cond(
        always,
        remaining,
        lambda *a: jax.tree.map(jnp.zeros_like, remaining(*a)),
        entering,
        arriving,
    )
    sent_back, following, rest = lax.optimization_barrier((sent_back, following, rest))
    decay_grad, step_grad, key_mine, query_mine, conv_grad = rest
    keys_grad = key_mine + sent_back[:, :half_width]
    queries_grad = query_mine + sent_back[:, half_width:]
    extended = jnp.concatenate([conv_grad, following], 0)
    input_grad = jnp.zeros_like(conv_grad)
    for offset in range(4):
        input_grad = (
            input_grad + conv_weight[offset][None, :] * extended[3 - offset : 3 - offset + length]
        )
    return (input_grad.astype(jnp.bfloat16), keys_grad, queries_grad, decay_grad, step_grad)


def solution(mesh):
    return jax.shard_map(
        body,
        mesh=mesh,
        in_specs=(
            P("seq", "head"),
            P("seq", "head"),
            P("seq", "head"),
            P("seq", "head"),
            P("seq", "head"),
            P("seq", "head"),
            P("head"),
            P(None, "head"),
        ),
        out_specs=(
            P("seq", "head"),
            P("seq", "head"),
            P("seq", "head"),
            P("seq", "head"),
            P("seq", "head"),
        ),
        check_vma=False,
    )
```

```python
import jax
import jax.numpy as jnp
from jax import lax
from jax.sharding import PartitionSpec as P

precise = lax.Precision.HIGHEST


def swapped(block, axis, bit):
    count = lax.axis_size(axis)
    route = []
    for low in range(count):
        high = low | 1 << bit
        if high != low and high < count:
            route += [(low, high), (high, low)]
    return lax.ppermute(block, axis, route)


def scanned_in(shards, axis):
    peers = lax.axis_size(axis)
    near = [(jnp.ones_like(a), jnp.zeros_like(s)) for a, s, _ in shards]
    window = [(a, s) for a, s, _ in shards]
    distance = 1
    while distance < peers:
        routes = []
        for _, _, reverse in shards:
            step = -distance if reverse else distance
            routes.append([(i, i + step) for i in range(peers) if 0 <= i + step < peers])
        received = [lax.ppermute(w, axis, r) for w, r in zip(window, routes)]
        more = 2 * distance < peers
        for k, (far_a, far_s) in enumerate(received):
            near_a, near_s = near[k]
            near[k] = (near_a * far_a, near_s + near_a[:, None, None] * far_s)
            if more:
                win_a, win_s = window[k]
                window[k] = (win_a * far_a, win_s + win_a[:, None, None] * far_s)
        distance *= 2
    return [s for _, s in near]


def packed(decay, state, kind):
    heads, width = state.shape[0], state.shape[1]
    if kind == jnp.float32:
        parts = decay
    else:
        high = decay.astype(kind)
        parts = jnp.concatenate([high, (decay - high.astype(decay.dtype)).astype(kind)])
    row = jnp.pad(parts.astype(kind), (0, width - parts.shape[0]))
    slab = jnp.broadcast_to(row[None, :, None], (1,) + state.shape[1:])
    return jnp.concatenate([state.astype(kind), slab], 0)


def unpacked(message):
    heads = message.shape[0] - 1
    row = message[heads, :, 0].astype(jnp.float32)
    decay = row[:heads] if message.dtype == jnp.float32 else row[:heads] + row[heads : 2 * heads]
    return decay, message[:heads].astype(jnp.float32)


def paired_scan(decay, state, state_grad, axis, rider_fn, rider_inputs):
    peers = lax.axis_size(axis)
    if peers % 2:
        found = scanned_in([(decay, state, False), (decay, state_grad, True)], axis)
        return found[0], found[1], rider_fn(*rider_inputs)
    is_odd = lax.axis_index(axis) % 2 == 1
    swap = [(i, i ^ 1) for i in range(peers)]
    sent = jnp.where(is_odd, state_grad, state)
    message = packed(decay, sent, jnp.bfloat16)
    if peers == 2:
        message, rider_inputs = lax.optimization_barrier((message, rider_inputs))
        riders = rider_fn(*rider_inputs)
    mate = lax.ppermute(message, axis, swap)
    if peers == 2:
        mate, riders = lax.optimization_barrier((mate, riders))
    mate_a, mate_s = unpacked(mate)
    own = jnp.where(is_odd, state, state_grad)
    window = (decay * mate_a, own + decay[:, None, None] * mate_s)
    near = (jnp.ones_like(decay), jnp.zeros_like(own))
    distance = 2
    while distance < peers:
        route = [(i, i + distance) for i in range(1, peers, 2) if i + distance < peers]
        route += [(i, i - distance) for i in range(0, peers, 2) if i - distance >= 0]
        if 2 * distance >= peers:
            far_s = lax.ppermute(window[1].astype(jnp.bfloat16), axis, route)
            if distance == 2:
                far_s, rider_inputs = lax.optimization_barrier((far_s, rider_inputs))
                riders = rider_fn(*rider_inputs)
            near = (near[0], near[1] + near[0][:, None, None] * far_s.astype(jnp.float32))
        else:
            far = lax.ppermute(packed(*window, jnp.bfloat16), axis, route)
            if distance == 2:
                far, rider_inputs = lax.optimization_barrier((far, rider_inputs))
                riders = rider_fn(*rider_inputs)
            far_a, far_s = unpacked(far)
            near = (near[0] * far_a, near[1] + near[0][:, None, None] * far_s)
            window = (window[0] * far_a, window[1] + window[0][:, None, None] * far_s)
        distance *= 2
    passing, riders = lax.optimization_barrier((near[1], riders))
    handed = lax.ppermute(passing.astype(jnp.bfloat16), axis, swap).astype(jnp.float32)
    mine = mate_s + mate_a[:, None, None] * near[1]
    return jnp.where(is_odd, mine, handed), jnp.where(is_odd, handed, mine), riders


def shifted(block, axis, distance):
    devices = range(lax.axis_size(axis))
    route = [(i - distance, i) for i in devices if i - distance in devices]
    return lax.ppermute(block, axis, route)


def product(left, right):
    return jnp.dot(left, right, preferred_element_type=jnp.float32, precision=precise)


def body(
    conv_output, output_grad, write_keys, read_queries, log_decay, step_size, skip_gain, conv_weight
):
    length = conv_output.shape[0]
    head_count = log_decay.shape[1]
    head_width = conv_output.shape[1] // head_count
    parity = lax.axis_index("head") % 2
    own_first = parity == 0
    half = write_keys.shape[1]
    both = swapped(jnp.concatenate([write_keys, read_queries], 1), "head", 0)
    partner = (both[:, :half], both[:, half:])
    keys_full = jnp.where(
        own_first,
        jnp.concatenate([write_keys, partner[0]], 1),
        jnp.concatenate([partner[0], write_keys], 1),
    ).astype(jnp.float32)
    queries_full = jnp.where(
        own_first,
        jnp.concatenate([read_queries, partner[1]], 1),
        jnp.concatenate([partner[1], read_queries], 1),
    ).astype(jnp.float32)
    state_count = keys_full.shape[1]
    preact = conv_output.astype(jnp.float32)
    values = jax.nn.silu(preact)
    upstream = output_grad.astype(jnp.float32)
    values3 = values.reshape(length, head_count, head_width)
    upstream3 = upstream.reshape(length, head_count, head_width)
    cumulative = jnp.cumsum(log_decay, axis=0)
    totals = cumulative[-1]
    to_end = jnp.exp(totals[None, :] - cumulative)
    from_start = jnp.exp(cumulative)
    weighted = values3 * (to_end * step_size)[:, :, None]
    seeded = upstream3 * from_start[:, :, None]
    local_state = jnp.einsum("ln,lhp->hnp", keys_full, weighted, precision=precise)
    local_grad = jnp.einsum("ln,lhp->hnp", queries_full, seeded, precision=precise)
    decay_total = jnp.exp(totals)
    def local_terms(keys_full, queries_full, values3, upstream3, cumulative, step_size, preact):
        scores = product(queries_full, keys_full.T)
        row_ids = lax.broadcasted_iota(jnp.int32, (length, length), 0)
        col_ids = lax.broadcasted_iota(jnp.int32, (length, length), 1)
        causal = row_ids >= col_ids
        cum_heads = cumulative.T
        step_heads = step_size.T
        log_gap = jnp.where(causal[None], cum_heads[:, :, None] - cum_heads[:, None, :], -1e30)
        decay_mask = jnp.exp(log_gap)
        pair_dots = jnp.einsum("thp,shp->hts", upstream3, values3, precision=precise)
        masked_scores = decay_mask * scores[None]
        weight_sum = jnp.einsum("hts,hs->ts", decay_mask * pair_dots, step_heads, precision=precise)
        within = jnp.einsum(
            "hts,thp->shp", masked_scores * step_heads[:, None, :], upstream3, precision=precise
        )
        effect = masked_scores * pair_dots
        row_sums = jnp.einsum("hts,hs->th", effect, step_heads, precision=precise)
        col_sums = jnp.sum(effect, 1).T
        logistic = jax.nn.sigmoid(preact)
        return (
            within + skip_gain[None, :, None] * upstream3,
            row_sums - col_sums * step_size,
            col_sums,
            product(weight_sum, keys_full),
            lax.dot_general(
                weight_sum,
                queries_full,
                (((0,), (0,)), ((), ())),
                preferred_element_type=jnp.float32,
                precision=precise,
            ),
            logistic * (1.0 + preact * (1.0 - logistic)),
        )
    def local_block(*inputs):
        always = lax.axis_index("seq") >= 0
        return lax.cond(
            always,
            local_terms,
            lambda *a: jax.tree.map(jnp.zeros_like, local_terms(*a)),
            *inputs,
        )

    entering, arriving, riders = paired_scan(
        decay_total,
        local_state,
        local_grad,
        "seq",
        local_block,
        (keys_full, queries_full, values3, upstream3, cumulative, step_size, preact),
    )
    within_part, local_decay, col_sums, query_local, key_local, silu_slope = riders
    from_state = jnp.einsum("ln,hnp->lhp", queries_full, entering, precision=precise)
    into_state = jnp.einsum("ln,hnp->lhp", keys_full, arriving, precision=precise)
    carried = jnp.sum(values3 * into_state, 2)
    step_grad = col_sums + to_end * carried
    value_grad = within_part + (to_end * step_size)[:, :, None] * into_state
    leaving = decay_total[:, None, None] * entering + local_state
    decay_terms = (
        local_decay
        + from_start * jnp.sum(upstream3 * from_state, 2)
        - to_end * step_size * carried
    )
    last_row = (lax.broadcasted_iota(jnp.int32, (length, 1), 0) == length - 1).astype(jnp.float32)
    decay_terms = decay_terms + last_row * jnp.sum(arriving * leaving, (1, 2))[None, :]
    decay_grad = jnp.flip(jnp.cumsum(jnp.flip(decay_terms, 0), 0), 0)
    query_part = query_local + jnp.einsum(
        "lhp,hnp->ln", seeded, entering, precision=precise
    )
    key_part = key_local + jnp.einsum("lhp,hnp->ln", weighted, arriving, precision=precise)
    half_width = state_count // 2
    key_mine = jnp.where(own_first, key_part[:, :half_width], key_part[:, half_width:])
    key_other = jnp.where(own_first, key_part[:, half_width:], key_part[:, :half_width])
    query_mine = jnp.where(own_first, query_part[:, :half_width], query_part[:, half_width:])
    query_other = jnp.where(own_first, query_part[:, half_width:], query_part[:, :half_width])
    sent_back = swapped(
        jnp.concatenate([key_other, query_other], 1).astype(jnp.bfloat16), "head", 0
    ).astype(key_other.dtype)
    received = (sent_back[:, :half_width], sent_back[:, half_width:])
    keys_grad = key_mine + received[0]
    queries_grad = query_mine + received[1]
    conv_grad = value_grad.reshape(length, -1) * silu_slope
    following = shifted(conv_grad[:3], "seq", -1)
    extended = jnp.concatenate([conv_grad, following], 0)
    input_grad = jnp.zeros_like(conv_grad)
    for offset in range(4):
        input_grad = (
            input_grad + conv_weight[offset][None, :] * extended[3 - offset : 3 - offset + length]
        )
    return (input_grad.astype(jnp.bfloat16), keys_grad, queries_grad, decay_grad, step_grad)


def solution(mesh):
    return jax.shard_map(
        body,
        mesh=mesh,
        in_specs=(
            P("seq", "head"),
            P("seq", "head"),
            P("seq", "head"),
            P("seq", "head"),
            P("seq", "head"),
            P("seq", "head"),
            P("head"),
            P(None, "head"),
        ),
        out_specs=(
            P("seq", "head"),
            P("seq", "head"),
            P("seq", "head"),
            P("seq", "head"),
            P("seq", "head"),
        ),
        check_vma=False,
    )
```

```python
import jax
import jax.numpy as jnp
from jax import lax
from jax.sharding import PartitionSpec as P

precise = lax.Precision.HIGHEST


def swapped(block, axis, bit):
    count = lax.axis_size(axis)
    route = []
    for low in range(count):
        high = low | 1 << bit
        if high != low and high < count:
            route += [(low, high), (high, low)]
    return lax.ppermute(block, axis, route)


def scanned_in(shards, axis):
    peers = lax.axis_size(axis)
    near = [(jnp.ones_like(a), jnp.zeros_like(s)) for a, s, _ in shards]
    window = [(a, s) for a, s, _ in shards]
    distance = 1
    while distance < peers:
        routes = []
        for _, _, reverse in shards:
            step = -distance if reverse else distance
            routes.append([(i, i + step) for i in range(peers) if 0 <= i + step < peers])
        received = [lax.ppermute(w, axis, r) for w, r in zip(window, routes)]
        more = 2 * distance < peers
        for k, (far_a, far_s) in enumerate(received):
            near_a, near_s = near[k]
            near[k] = (near_a * far_a, near_s + near_a[:, None, None] * far_s)
            if more:
                win_a, win_s = window[k]
                window[k] = (win_a * far_a, win_s + win_a[:, None, None] * far_s)
        distance *= 2
    return [s for _, s in near]


def packed(decay, state, kind):
    heads, width = state.shape[0], state.shape[1]
    if kind == jnp.float32:
        parts = decay
    else:
        high = decay.astype(kind)
        parts = jnp.concatenate([high, (decay - high.astype(decay.dtype)).astype(kind)])
    row = jnp.pad(parts.astype(kind), (0, width - parts.shape[0]))
    slab = jnp.broadcast_to(row[None, :, None], (1,) + state.shape[1:])
    return jnp.concatenate([state.astype(kind), slab], 0)


def split_packed(decay, state):
    high = state.astype(jnp.bfloat16)
    low = (state - high.astype(state.dtype)).astype(jnp.bfloat16)
    return jnp.concatenate([high, low, packed(decay, state, jnp.bfloat16)[-1:]], 0)


def split_unpacked(message):
    heads = (message.shape[0] - 1) // 2
    row = message[2 * heads, :, 0].astype(jnp.float32)
    decay = row[:heads] + row[heads : 2 * heads]
    both = message[: 2 * heads].astype(jnp.float32)
    return decay, both[:heads] + both[heads:]


def unpacked(message):
    heads = message.shape[0] - 1
    row = message[heads, :, 0].astype(jnp.float32)
    decay = row[:heads] if message.dtype == jnp.float32 else row[:heads] + row[heads : 2 * heads]
    return decay, message[:heads].astype(jnp.float32)


def paired_scan(decay, state, state_grad, axis, rider_fn, rider_inputs):
    peers = lax.axis_size(axis)
    if peers % 2:
        found = scanned_in([(decay, state, False), (decay, state_grad, True)], axis)
        return found[0], found[1], rider_fn(*rider_inputs)
    is_odd = lax.axis_index(axis) % 2 == 1
    swap = [(i, i ^ 1) for i in range(peers)]
    sent = jnp.where(is_odd, state_grad, state)
    message = split_packed(decay, sent)
    if peers == 2:
        message, rider_inputs = lax.optimization_barrier((message, rider_inputs))
        riders = rider_fn(*rider_inputs)
    mate = lax.ppermute(message, axis, swap)
    if peers == 2:
        mate, riders = lax.optimization_barrier((mate, riders))
    mate_a, mate_s = split_unpacked(mate)
    own = jnp.where(is_odd, state, state_grad)
    window = (decay * mate_a, own + decay[:, None, None] * mate_s)
    near = (jnp.ones_like(decay), jnp.zeros_like(own))
    distance = 2
    while distance < peers:
        route = [(i, i + distance) for i in range(1, peers, 2) if i + distance < peers]
        route += [(i, i - distance) for i in range(0, peers, 2) if i - distance >= 0]
        if 2 * distance >= peers:
            far_s = lax.ppermute(window[1].astype(jnp.bfloat16), axis, route)
            if distance == 2:
                far_s, rider_inputs = lax.optimization_barrier((far_s, rider_inputs))
                riders = rider_fn(*rider_inputs)
            near = (near[0], near[1] + near[0][:, None, None] * far_s.astype(jnp.float32))
        else:
            far = lax.ppermute(packed(*window, jnp.bfloat16), axis, route)
            if distance == 2:
                far, rider_inputs = lax.optimization_barrier((far, rider_inputs))
                riders = rider_fn(*rider_inputs)
            far_a, far_s = unpacked(far)
            near = (near[0] * far_a, near[1] + near[0][:, None, None] * far_s)
            window = (window[0] * far_a, window[1] + window[0][:, None, None] * far_s)
        distance *= 2
    passing, riders = lax.optimization_barrier((near[1], riders))
    high = passing.astype(jnp.bfloat16)
    low = (passing - high.astype(passing.dtype)).astype(jnp.bfloat16)
    handed = lax.ppermute(jnp.concatenate([high, low], 0), axis, swap).astype(jnp.float32)
    handed = handed[: passing.shape[0]] + handed[passing.shape[0] :]
    mine = mate_s + mate_a[:, None, None] * near[1]
    return jnp.where(is_odd, mine, handed), jnp.where(is_odd, handed, mine), riders


def shifted(block, axis, distance):
    devices = range(lax.axis_size(axis))
    route = [(i - distance, i) for i in devices if i - distance in devices]
    return lax.ppermute(block, axis, route)


def product(left, right):
    return jnp.dot(left, right, preferred_element_type=jnp.float32, precision=precise)


def body(
    conv_output, output_grad, write_keys, read_queries, log_decay, step_size, skip_gain, conv_weight
):
    length = conv_output.shape[0]
    head_count = log_decay.shape[1]
    head_width = conv_output.shape[1] // head_count
    parity = lax.axis_index("head") % 2
    own_first = parity == 0
    half = write_keys.shape[1]
    both = swapped(jnp.concatenate([write_keys, read_queries], 1), "head", 0)
    partner = (both[:, :half], both[:, half:])
    keys_full = jnp.where(
        own_first,
        jnp.concatenate([write_keys, partner[0]], 1),
        jnp.concatenate([partner[0], write_keys], 1),
    ).astype(jnp.float32)
    queries_full = jnp.where(
        own_first,
        jnp.concatenate([read_queries, partner[1]], 1),
        jnp.concatenate([partner[1], read_queries], 1),
    ).astype(jnp.float32)
    state_count = keys_full.shape[1]
    preact = conv_output.astype(jnp.float32)
    values = jax.nn.silu(preact)
    upstream = output_grad.astype(jnp.float32)
    values3 = values.reshape(length, head_count, head_width)
    upstream3 = upstream.reshape(length, head_count, head_width)
    cumulative = jnp.cumsum(log_decay, axis=0)
    totals = cumulative[-1]
    to_end = jnp.exp(totals[None, :] - cumulative)
    from_start = jnp.exp(cumulative)
    weighted = values3 * (to_end * step_size)[:, :, None]
    seeded = upstream3 * from_start[:, :, None]
    local_state = jnp.einsum("ln,lhp->hnp", keys_full, weighted, precision=precise)
    local_grad = jnp.einsum("ln,lhp->hnp", queries_full, seeded, precision=precise)
    decay_total = jnp.exp(totals)
    def local_terms(keys_full, queries_full, values3, upstream3, cumulative, step_size, preact):
        scores = product(queries_full, keys_full.T)
        row_ids = lax.broadcasted_iota(jnp.int32, (length, length), 0)
        col_ids = lax.broadcasted_iota(jnp.int32, (length, length), 1)
        causal = row_ids >= col_ids
        cum_heads = cumulative.T
        step_heads = step_size.T
        log_gap = jnp.where(causal[None], cum_heads[:, :, None] - cum_heads[:, None, :], -1e30)
        decay_mask = jnp.exp(log_gap)
        pair_dots = jnp.einsum("thp,shp->hts", upstream3, values3, precision=precise)
        masked_scores = decay_mask * scores[None]
        weight_sum = jnp.einsum("hts,hs->ts", decay_mask * pair_dots, step_heads, precision=precise)
        within = jnp.einsum(
            "hts,thp->shp", masked_scores * step_heads[:, None, :], upstream3, precision=precise
        )
        effect = masked_scores * pair_dots
        row_sums = jnp.einsum("hts,hs->th", effect, step_heads, precision=precise)
        col_sums = jnp.sum(effect, 1).T
        logistic = jax.nn.sigmoid(preact)
        return (
            within + skip_gain[None, :, None] * upstream3,
            row_sums - col_sums * step_size,
            col_sums,
            product(weight_sum, keys_full),
            lax.dot_general(
                weight_sum,
                queries_full,
                (((0,), (0,)), ((), ())),
                preferred_element_type=jnp.float32,
                precision=precise,
            ),
            logistic * (1.0 + preact * (1.0 - logistic)),
        )
    def local_block(*inputs):
        always = lax.axis_index("seq") >= 0
        return lax.cond(
            always,
            local_terms,
            lambda *a: jax.tree.map(jnp.zeros_like, local_terms(*a)),
            *inputs,
        )

    entering, arriving, riders = paired_scan(
        decay_total,
        local_state,
        local_grad,
        "seq",
        local_block,
        (keys_full, queries_full, values3, upstream3, cumulative, step_size, preact),
    )
    within_part, local_decay, col_sums, query_local, key_local, silu_slope = riders
    from_state = jnp.einsum("ln,hnp->lhp", queries_full, entering, precision=precise)
    into_state = jnp.einsum("ln,hnp->lhp", keys_full, arriving, precision=precise)
    carried = jnp.sum(values3 * into_state, 2)
    step_grad = col_sums + to_end * carried
    value_grad = within_part + (to_end * step_size)[:, :, None] * into_state
    leaving = decay_total[:, None, None] * entering + local_state
    decay_terms = (
        local_decay
        + from_start * jnp.sum(upstream3 * from_state, 2)
        - to_end * step_size * carried
    )
    last_row = (lax.broadcasted_iota(jnp.int32, (length, 1), 0) == length - 1).astype(jnp.float32)
    decay_terms = decay_terms + last_row * jnp.sum(arriving * leaving, (1, 2))[None, :]
    decay_grad = jnp.flip(jnp.cumsum(jnp.flip(decay_terms, 0), 0), 0)
    query_part = query_local + jnp.einsum(
        "lhp,hnp->ln", seeded, entering, precision=precise
    )
    key_part = key_local + jnp.einsum("lhp,hnp->ln", weighted, arriving, precision=precise)
    half_width = state_count // 2
    key_mine = jnp.where(own_first, key_part[:, :half_width], key_part[:, half_width:])
    key_other = jnp.where(own_first, key_part[:, half_width:], key_part[:, :half_width])
    query_mine = jnp.where(own_first, query_part[:, :half_width], query_part[:, half_width:])
    query_other = jnp.where(own_first, query_part[:, half_width:], query_part[:, :half_width])
    sent_back = swapped(
        jnp.concatenate([key_other, query_other], 1).astype(jnp.bfloat16), "head", 0
    ).astype(key_other.dtype)
    received = (sent_back[:, :half_width], sent_back[:, half_width:])
    keys_grad = key_mine + received[0]
    queries_grad = query_mine + received[1]
    conv_grad = value_grad.reshape(length, -1) * silu_slope
    following = shifted(conv_grad[:3], "seq", -1)
    extended = jnp.concatenate([conv_grad, following], 0)
    input_grad = jnp.zeros_like(conv_grad)
    for offset in range(4):
        input_grad = (
            input_grad + conv_weight[offset][None, :] * extended[3 - offset : 3 - offset + length]
        )
    return (input_grad.astype(jnp.bfloat16), keys_grad, queries_grad, decay_grad, step_grad)


def solution(mesh):
    return jax.shard_map(
        body,
        mesh=mesh,
        in_specs=(
            P("seq", "head"),
            P("seq", "head"),
            P("seq", "head"),
            P("seq", "head"),
            P("seq", "head"),
            P("seq", "head"),
            P("head"),
            P(None, "head"),
        ),
        out_specs=(
            P("seq", "head"),
            P("seq", "head"),
            P("seq", "head"),
            P("seq", "head"),
            P("seq", "head"),
        ),
        check_vma=False,
    )
```

```python
import jax
import jax.numpy as jnp
from jax import lax
from jax.sharding import PartitionSpec as P

precise = lax.Precision.HIGHEST


def swapped(block, axis, bit):
    count = lax.axis_size(axis)
    route = []
    for low in range(count):
        high = low | 1 << bit
        if high != low and high < count:
            route += [(low, high), (high, low)]
    return lax.ppermute(block, axis, route)


def scanned_in(shards, axis):
    peers = lax.axis_size(axis)
    near = [(jnp.ones_like(a), jnp.zeros_like(s)) for a, s, _ in shards]
    window = [(a, s) for a, s, _ in shards]
    distance = 1
    while distance < peers:
        routes = []
        for _, _, reverse in shards:
            step = -distance if reverse else distance
            routes.append([(i, i + step) for i in range(peers) if 0 <= i + step < peers])
        received = [lax.ppermute(w, axis, r) for w, r in zip(window, routes)]
        more = 2 * distance < peers
        for k, (far_a, far_s) in enumerate(received):
            near_a, near_s = near[k]
            near[k] = (near_a * far_a, near_s + near_a[:, None, None] * far_s)
            if more:
                win_a, win_s = window[k]
                window[k] = (win_a * far_a, win_s + win_a[:, None, None] * far_s)
        distance *= 2
    return [s for _, s in near]


def packed(decay, state, kind):
    heads, width = state.shape[0], state.shape[1]
    if kind == jnp.float32:
        parts = decay
    else:
        high = decay.astype(kind)
        parts = jnp.concatenate([high, (decay - high.astype(decay.dtype)).astype(kind)])
    row = jnp.pad(parts.astype(kind), (0, width - parts.shape[0]))
    slab = jnp.broadcast_to(row[None, :, None], (1,) + state.shape[1:])
    return jnp.concatenate([state.astype(kind), slab], 0)


def unpacked(message):
    heads = message.shape[0] - 1
    row = message[heads, :, 0].astype(jnp.float32)
    decay = row[:heads] if message.dtype == jnp.float32 else row[:heads] + row[heads : 2 * heads]
    return decay, message[:heads].astype(jnp.float32)


def paired_scan(decay, state, state_grad, axis, rider_fn, rider_inputs):
    peers = lax.axis_size(axis)
    if peers % 2:
        found = scanned_in([(decay, state, False), (decay, state_grad, True)], axis)
        return found[0], found[1], rider_fn(*rider_inputs)
    is_odd = lax.axis_index(axis) % 2 == 1
    swap = [(i, i ^ 1) for i in range(peers)]
    sent = jnp.where(is_odd, state_grad, state)
    message = packed(decay, sent, jnp.float32)
    if peers == 2:
        message, rider_inputs = lax.optimization_barrier((message, rider_inputs))
        riders = rider_fn(*rider_inputs)
    mate = lax.ppermute(message, axis, swap)
    if peers == 2:
        mate, riders = lax.optimization_barrier((mate, riders))
    mate_a, mate_s = unpacked(mate)
    own = jnp.where(is_odd, state, state_grad)
    window = (decay * mate_a, own + decay[:, None, None] * mate_s)
    near = (jnp.ones_like(decay), jnp.zeros_like(own))
    distance = 2
    while distance < peers:
        route = [(i, i + distance) for i in range(1, peers, 2) if i + distance < peers]
        route += [(i, i - distance) for i in range(0, peers, 2) if i - distance >= 0]
        if 2 * distance >= peers:
            far_s = lax.ppermute(window[1].astype(jnp.bfloat16), axis, route)
            if distance == 2:
                far_s, rider_inputs = lax.optimization_barrier((far_s, rider_inputs))
                riders = rider_fn(*rider_inputs)
            near = (near[0], near[1] + near[0][:, None, None] * far_s.astype(jnp.float32))
        else:
            far = lax.ppermute(packed(*window, jnp.bfloat16), axis, route)
            if distance == 2:
                far, rider_inputs = lax.optimization_barrier((far, rider_inputs))
                riders = rider_fn(*rider_inputs)
            far_a, far_s = unpacked(far)
            near = (near[0] * far_a, near[1] + near[0][:, None, None] * far_s)
            window = (window[0] * far_a, window[1] + window[0][:, None, None] * far_s)
        distance *= 2
    passing, riders = lax.optimization_barrier((near[1], riders))
    handed = lax.ppermute(passing, axis, swap)
    mine = mate_s + mate_a[:, None, None] * near[1]
    return jnp.where(is_odd, mine, handed), jnp.where(is_odd, handed, mine), riders


def shifted(block, axis, distance):
    devices = range(lax.axis_size(axis))
    route = [(i - distance, i) for i in devices if i - distance in devices]
    return lax.ppermute(block, axis, route)


def product(left, right):
    return jnp.dot(left, right, preferred_element_type=jnp.float32, precision=precise)


def body(
    conv_output, output_grad, write_keys, read_queries, log_decay, step_size, skip_gain, conv_weight
):
    length = conv_output.shape[0]
    head_count = log_decay.shape[1]
    head_width = conv_output.shape[1] // head_count
    parity = lax.axis_index("head") % 2
    own_first = parity == 0
    half = write_keys.shape[1]
    both = swapped(jnp.concatenate([write_keys, read_queries], 1), "head", 0)
    partner = (both[:, :half], both[:, half:])
    keys_full = jnp.where(
        own_first,
        jnp.concatenate([write_keys, partner[0]], 1),
        jnp.concatenate([partner[0], write_keys], 1),
    ).astype(jnp.float32)
    queries_full = jnp.where(
        own_first,
        jnp.concatenate([read_queries, partner[1]], 1),
        jnp.concatenate([partner[1], read_queries], 1),
    ).astype(jnp.float32)
    state_count = keys_full.shape[1]
    preact = conv_output.astype(jnp.float32)
    values = jax.nn.silu(preact)
    upstream = output_grad.astype(jnp.float32)
    values3 = values.reshape(length, head_count, head_width)
    upstream3 = upstream.reshape(length, head_count, head_width)
    token_row = lax.broadcasted_iota(jnp.int32, (length, length), 0)
    token_col = lax.broadcasted_iota(jnp.int32, (length, length), 1)
    cumulative = product((token_row >= token_col).astype(jnp.float32), log_decay)
    totals = cumulative[-1]
    to_end = jnp.exp(totals[None, :] - cumulative)
    from_start = jnp.exp(cumulative)
    weighted = values3 * (to_end * step_size)[:, :, None]
    seeded = upstream3 * from_start[:, :, None]
    local_state = jnp.einsum("ln,lhp->hnp", keys_full, weighted, precision=precise)
    local_grad = jnp.einsum("ln,lhp->hnp", queries_full, seeded, precision=precise)
    decay_total = jnp.exp(totals)
    def local_terms(keys_full, queries_full, values3, upstream3, cumulative, step_size, preact):
        scores = product(queries_full, keys_full.T)
        row_ids = lax.broadcasted_iota(jnp.int32, (length, length), 0)
        col_ids = lax.broadcasted_iota(jnp.int32, (length, length), 1)
        causal = row_ids >= col_ids
        cum_heads = cumulative.T
        step_heads = step_size.T
        log_gap = jnp.where(causal[None], cum_heads[:, :, None] - cum_heads[:, None, :], -1e30)
        decay_mask = jnp.exp(log_gap)
        pair_dots = jnp.einsum("thp,shp->hts", upstream3, values3, precision=precise)
        masked_scores = decay_mask * scores[None]
        weight_sum = jnp.einsum("hts,hs->ts", decay_mask * pair_dots, step_heads, precision=precise)
        within = jnp.einsum(
            "hts,thp->shp", masked_scores * step_heads[:, None, :], upstream3, precision=precise
        )
        effect = masked_scores * pair_dots
        row_sums = jnp.einsum("hts,hs->th", effect, step_heads, precision=precise)
        col_sums = jnp.sum(effect, 1).T
        logistic = jax.nn.sigmoid(preact)
        return (
            within + skip_gain[None, :, None] * upstream3,
            row_sums - col_sums * step_size,
            col_sums,
            product(weight_sum, keys_full),
            lax.dot_general(
                weight_sum,
                queries_full,
                (((0,), (0,)), ((), ())),
                preferred_element_type=jnp.float32,
                precision=precise,
            ),
            logistic * (1.0 + preact * (1.0 - logistic)),
        )
    def local_block(*inputs):
        always = lax.axis_index("seq") >= 0
        return lax.cond(
            always,
            local_terms,
            lambda *a: jax.tree.map(jnp.zeros_like, local_terms(*a)),
            *inputs,
        )

    entering, arriving, riders = paired_scan(
        decay_total,
        local_state,
        local_grad,
        "seq",
        local_block,
        (keys_full, queries_full, values3, upstream3, cumulative, step_size, preact),
    )
    within_part, local_decay, col_sums, query_local, key_local, silu_slope = riders
    from_state = jnp.einsum("ln,hnp->lhp", queries_full, entering, precision=precise)
    into_state = jnp.einsum("ln,hnp->lhp", keys_full, arriving, precision=precise)
    carried = jnp.sum(values3 * into_state, 2)
    step_grad = col_sums + to_end * carried
    value_grad = within_part + (to_end * step_size)[:, :, None] * into_state
    leaving = decay_total[:, None, None] * entering + local_state
    decay_terms = (
        local_decay
        + from_start * jnp.sum(upstream3 * from_state, 2)
        - to_end * step_size * carried
    )
    last_row = (lax.broadcasted_iota(jnp.int32, (length, 1), 0) == length - 1).astype(jnp.float32)
    decay_terms = decay_terms + last_row * jnp.sum(arriving * leaving, (1, 2))[None, :]
    decay_grad = product((token_row <= token_col).astype(jnp.float32), decay_terms)
    query_part = query_local + jnp.einsum(
        "lhp,hnp->ln", seeded, entering, precision=precise
    )
    key_part = key_local + jnp.einsum("lhp,hnp->ln", weighted, arriving, precision=precise)
    half_width = state_count // 2
    key_mine = jnp.where(own_first, key_part[:, :half_width], key_part[:, half_width:])
    key_other = jnp.where(own_first, key_part[:, half_width:], key_part[:, :half_width])
    query_mine = jnp.where(own_first, query_part[:, :half_width], query_part[:, half_width:])
    query_other = jnp.where(own_first, query_part[:, half_width:], query_part[:, :half_width])
    sent_back = swapped(
        jnp.concatenate([key_other, query_other], 1).astype(jnp.bfloat16), "head", 0
    ).astype(key_other.dtype)
    received = (sent_back[:, :half_width], sent_back[:, half_width:])
    keys_grad = key_mine + received[0]
    queries_grad = query_mine + received[1]
    conv_grad = value_grad.reshape(length, -1) * silu_slope
    following = shifted(conv_grad[:3], "seq", -1)
    extended = jnp.concatenate([conv_grad, following], 0)
    input_grad = jnp.zeros_like(conv_grad)
    for offset in range(4):
        input_grad = (
            input_grad + conv_weight[offset][None, :] * extended[3 - offset : 3 - offset + length]
        )
    return (input_grad.astype(jnp.bfloat16), keys_grad, queries_grad, decay_grad, step_grad)


def solution(mesh):
    return jax.shard_map(
        body,
        mesh=mesh,
        in_specs=(
            P("seq", "head"),
            P("seq", "head"),
            P("seq", "head"),
            P("seq", "head"),
            P("seq", "head"),
            P("seq", "head"),
            P("head"),
            P(None, "head"),
        ),
        out_specs=(
            P("seq", "head"),
            P("seq", "head"),
            P("seq", "head"),
            P("seq", "head"),
            P("seq", "head"),
        ),
        check_vma=False,
    )
```

```python
import jax
import jax.numpy as jnp
from jax import lax
from jax.sharding import PartitionSpec as P

precise = lax.Precision.HIGHEST


def swapped(block, axis, bit):
    count = lax.axis_size(axis)
    route = []
    for low in range(count):
        high = low | 1 << bit
        if high != low and high < count:
            route += [(low, high), (high, low)]
    return lax.ppermute(block, axis, route)


def scanned_in(shards, axis):
    peers = lax.axis_size(axis)
    near = [(jnp.ones_like(a), jnp.zeros_like(s)) for a, s, _ in shards]
    window = [(a, s) for a, s, _ in shards]
    distance = 1
    while distance < peers:
        routes = []
        for _, _, reverse in shards:
            step = -distance if reverse else distance
            routes.append([(i, i + step) for i in range(peers) if 0 <= i + step < peers])
        received = [lax.ppermute(w, axis, r) for w, r in zip(window, routes)]
        more = 2 * distance < peers
        for k, (far_a, far_s) in enumerate(received):
            near_a, near_s = near[k]
            near[k] = (near_a * far_a, near_s + near_a[:, None, None] * far_s)
            if more:
                win_a, win_s = window[k]
                window[k] = (win_a * far_a, win_s + win_a[:, None, None] * far_s)
        distance *= 2
    return [s for _, s in near]


def packed(decay, state, kind):
    heads, width = state.shape[0], state.shape[1]
    if kind == jnp.float32:
        parts = decay
    else:
        high = decay.astype(kind)
        parts = jnp.concatenate([high, (decay - high.astype(decay.dtype)).astype(kind)])
    row = jnp.pad(parts.astype(kind), (0, width - parts.shape[0]))
    slab = jnp.broadcast_to(row[None, :, None], (1,) + state.shape[1:])
    return jnp.concatenate([state.astype(kind), slab], 0)


def unpacked(message):
    heads = message.shape[0] - 1
    row = message[heads, :, 0].astype(jnp.float32)
    decay = row[:heads] if message.dtype == jnp.float32 else row[:heads] + row[heads : 2 * heads]
    return decay, message[:heads].astype(jnp.float32)


def paired_scan(decay, state, state_grad, axis, rider_fn, rider_inputs):
    peers = lax.axis_size(axis)
    if peers % 2:
        found = scanned_in([(decay, state, False), (decay, state_grad, True)], axis)
        return found[0], found[1], rider_fn(*rider_inputs)
    is_odd = lax.axis_index(axis) % 2 == 1
    swap = [(i, i ^ 1) for i in range(peers)]
    sent = jnp.where(is_odd, state_grad, state)
    message = packed(decay, sent, jnp.float32)
    if peers == 2:
        message, rider_inputs = lax.optimization_barrier((message, rider_inputs))
        riders = rider_fn(*rider_inputs)
    mate = lax.ppermute(message, axis, swap)
    if peers == 2:
        mate, riders = lax.optimization_barrier((mate, riders))
    mate_a, mate_s = unpacked(mate)
    own = jnp.where(is_odd, state, state_grad)
    window = (decay * mate_a, own + decay[:, None, None] * mate_s)
    near = (jnp.ones_like(decay), jnp.zeros_like(own))
    distance = 2
    while distance < peers:
        route = [(i, i + distance) for i in range(1, peers, 2) if i + distance < peers]
        route += [(i, i - distance) for i in range(0, peers, 2) if i - distance >= 0]
        if 2 * distance >= peers:
            far_s = lax.ppermute(window[1].astype(jnp.bfloat16), axis, route)
            if distance == 2:
                far_s, rider_inputs = lax.optimization_barrier((far_s, rider_inputs))
                riders = rider_fn(*rider_inputs)
            near = (near[0], near[1] + near[0][:, None, None] * far_s.astype(jnp.float32))
        else:
            far = lax.ppermute(packed(*window, jnp.bfloat16), axis, route)
            if distance == 2:
                far, rider_inputs = lax.optimization_barrier((far, rider_inputs))
                riders = rider_fn(*rider_inputs)
            far_a, far_s = unpacked(far)
            near = (near[0] * far_a, near[1] + near[0][:, None, None] * far_s)
            window = (window[0] * far_a, window[1] + window[0][:, None, None] * far_s)
        distance *= 2
    passing, riders = lax.optimization_barrier((near[1], riders))
    handed = lax.ppermute(passing, axis, swap)
    mine = mate_s + mate_a[:, None, None] * near[1]
    return jnp.where(is_odd, mine, handed), jnp.where(is_odd, handed, mine), riders


def shifted(block, axis, distance):
    devices = range(lax.axis_size(axis))
    route = [(i - distance, i) for i in devices if i - distance in devices]
    return lax.ppermute(block, axis, route)


def product(left, right):
    return jnp.dot(left, right, preferred_element_type=jnp.float32, precision=precise)


def body(
    conv_output, output_grad, write_keys, read_queries, log_decay, step_size, skip_gain, conv_weight
):
    length = conv_output.shape[0]
    head_count = log_decay.shape[1]
    head_width = conv_output.shape[1] // head_count
    parity = lax.axis_index("head") % 2
    own_first = parity == 0
    half = write_keys.shape[1]
    mine_both = lax.optimization_barrier(jnp.concatenate([write_keys, read_queries], 1))
    both = swapped(mine_both, "head", 0)
    partner = (both[:, :half], both[:, half:])
    write_keys, read_queries = mine_both[:, :half], mine_both[:, half:]
    keys_full = jnp.where(
        own_first,
        jnp.concatenate([write_keys, partner[0]], 1),
        jnp.concatenate([partner[0], write_keys], 1),
    ).astype(jnp.float32)
    queries_full = jnp.where(
        own_first,
        jnp.concatenate([read_queries, partner[1]], 1),
        jnp.concatenate([partner[1], read_queries], 1),
    ).astype(jnp.float32)
    state_count = keys_full.shape[1]
    preact = conv_output.astype(jnp.float32)
    values = jax.nn.silu(preact)
    upstream = output_grad.astype(jnp.float32)
    values3 = values.reshape(length, head_count, head_width)
    upstream3 = upstream.reshape(length, head_count, head_width)
    token_row = lax.broadcasted_iota(jnp.int32, (length, length), 0)
    token_col = lax.broadcasted_iota(jnp.int32, (length, length), 1)
    cumulative = product((token_row >= token_col).astype(jnp.float32), log_decay)
    totals = cumulative[-1]
    to_end = jnp.exp(totals[None, :] - cumulative)
    from_start = jnp.exp(cumulative)
    weighted = values3 * (to_end * step_size)[:, :, None]
    seeded = upstream3 * from_start[:, :, None]
    local_state = jnp.einsum("ln,lhp->hnp", keys_full, weighted, precision=precise)
    local_grad = jnp.einsum("ln,lhp->hnp", queries_full, seeded, precision=precise)
    decay_total = jnp.exp(totals)
    def local_terms(keys_full, queries_full, values3, upstream3, cumulative, step_size, preact):
        scores = product(queries_full, keys_full.T)
        row_ids = lax.broadcasted_iota(jnp.int32, (length, length), 0)
        col_ids = lax.broadcasted_iota(jnp.int32, (length, length), 1)
        causal = row_ids >= col_ids
        cum_heads = cumulative.T
        step_heads = step_size.T
        log_gap = jnp.where(causal[None], cum_heads[:, :, None] - cum_heads[:, None, :], -1e30)
        decay_mask = jnp.exp(log_gap)
        pair_dots = jnp.einsum("thp,shp->hts", upstream3, values3, precision=precise)
        masked_scores = decay_mask * scores[None]
        weight_sum = jnp.einsum("hts,hs->ts", decay_mask * pair_dots, step_heads, precision=precise)
        within = jnp.einsum(
            "hts,thp->shp", masked_scores * step_heads[:, None, :], upstream3, precision=precise
        )
        effect = masked_scores * pair_dots
        row_sums = jnp.einsum("hts,hs->th", effect, step_heads, precision=precise)
        col_sums = jnp.sum(effect, 1).T
        logistic = jax.nn.sigmoid(preact)
        return (
            within + skip_gain[None, :, None] * upstream3,
            row_sums - col_sums * step_size,
            col_sums,
            product(weight_sum, keys_full),
            lax.dot_general(
                weight_sum,
                queries_full,
                (((0,), (0,)), ((), ())),
                preferred_element_type=jnp.float32,
                precision=precise,
            ),
            logistic * (1.0 + preact * (1.0 - logistic)),
        )
    def local_block(*inputs):
        always = lax.axis_index("seq") >= 0
        return lax.cond(
            always,
            local_terms,
            lambda *a: jax.tree.map(jnp.zeros_like, local_terms(*a)),
            *inputs,
        )

    entering, arriving, riders = paired_scan(
        decay_total,
        local_state,
        local_grad,
        "seq",
        local_block,
        (keys_full, queries_full, values3, upstream3, cumulative, step_size, preact),
    )
    within_part, local_decay, col_sums, query_local, key_local, silu_slope = riders
    from_state = jnp.einsum("ln,hnp->lhp", queries_full, entering, precision=precise)
    into_state = jnp.einsum("ln,hnp->lhp", keys_full, arriving, precision=precise)
    carried = jnp.sum(values3 * into_state, 2)
    step_grad = col_sums + to_end * carried
    value_grad = within_part + (to_end * step_size)[:, :, None] * into_state
    leaving = decay_total[:, None, None] * entering + local_state
    decay_terms = (
        local_decay
        + from_start * jnp.sum(upstream3 * from_state, 2)
        - to_end * step_size * carried
    )
    last_row = (lax.broadcasted_iota(jnp.int32, (length, 1), 0) == length - 1).astype(jnp.float32)
    decay_terms = decay_terms + last_row * jnp.sum(arriving * leaving, (1, 2))[None, :]
    decay_grad = product((token_row <= token_col).astype(jnp.float32), decay_terms)
    query_part = query_local + jnp.einsum(
        "lhp,hnp->ln", seeded, entering, precision=precise
    )
    key_part = key_local + jnp.einsum("lhp,hnp->ln", weighted, arriving, precision=precise)
    half_width = state_count // 2
    key_mine = jnp.where(own_first, key_part[:, :half_width], key_part[:, half_width:])
    key_other = jnp.where(own_first, key_part[:, half_width:], key_part[:, :half_width])
    query_mine = jnp.where(own_first, query_part[:, :half_width], query_part[:, half_width:])
    query_other = jnp.where(own_first, query_part[:, half_width:], query_part[:, :half_width])
    sent_back = swapped(
        jnp.concatenate([key_other, query_other], 1).astype(jnp.bfloat16), "head", 0
    ).astype(key_other.dtype)
    received = (sent_back[:, :half_width], sent_back[:, half_width:])
    keys_grad = key_mine + received[0]
    queries_grad = query_mine + received[1]
    conv_grad = value_grad.reshape(length, -1) * silu_slope
    following = shifted(conv_grad[:3], "seq", -1)
    extended = jnp.concatenate([conv_grad, following], 0)
    input_grad = jnp.zeros_like(conv_grad)
    for offset in range(4):
        input_grad = (
            input_grad + conv_weight[offset][None, :] * extended[3 - offset : 3 - offset + length]
        )
    return (input_grad.astype(jnp.bfloat16), keys_grad, queries_grad, decay_grad, step_grad)


def solution(mesh):
    return jax.shard_map(
        body,
        mesh=mesh,
        in_specs=(
            P("seq", "head"),
            P("seq", "head"),
            P("seq", "head"),
            P("seq", "head"),
            P("seq", "head"),
            P("seq", "head"),
            P("head"),
            P(None, "head"),
        ),
        out_specs=(
            P("seq", "head"),
            P("seq", "head"),
            P("seq", "head"),
            P("seq", "head"),
            P("seq", "head"),
        ),
        check_vma=False,
    )
```

```python
import jax
import jax.numpy as jnp
from jax import lax
from jax.sharding import PartitionSpec as P

precise = lax.Precision.HIGHEST


def swapped(block, axis, bit):
    count = lax.axis_size(axis)
    route = []
    for low in range(count):
        high = low | 1 << bit
        if high != low and high < count:
            route += [(low, high), (high, low)]
    return lax.ppermute(block, axis, route)


def scanned_in(shards, axis):
    peers = lax.axis_size(axis)
    near = [(jnp.ones_like(a), jnp.zeros_like(s)) for a, s, _ in shards]
    window = [(a, s) for a, s, _ in shards]
    distance = 1
    while distance < peers:
        routes = []
        for _, _, reverse in shards:
            step = -distance if reverse else distance
            routes.append([(i, i + step) for i in range(peers) if 0 <= i + step < peers])
        received = [lax.ppermute(w, axis, r) for w, r in zip(window, routes)]
        more = 2 * distance < peers
        for k, (far_a, far_s) in enumerate(received):
            near_a, near_s = near[k]
            near[k] = (near_a * far_a, near_s + near_a[:, None, None] * far_s)
            if more:
                win_a, win_s = window[k]
                window[k] = (win_a * far_a, win_s + win_a[:, None, None] * far_s)
        distance *= 2
    return [s for _, s in near]


def packed(decay, state, kind):
    heads, width = state.shape[0], state.shape[1]
    if kind == jnp.float32:
        parts = decay
    else:
        high = decay.astype(kind)
        parts = jnp.concatenate([high, (decay - high.astype(decay.dtype)).astype(kind)])
    row = jnp.pad(parts.astype(kind), (0, width - parts.shape[0]))
    slab = jnp.broadcast_to(row[None, :, None], (1,) + state.shape[1:])
    return jnp.concatenate([state.astype(kind), slab], 0)


def unpacked(message):
    heads = message.shape[0] - 1
    row = message[heads, :, 0].astype(jnp.float32)
    decay = row[:heads] if message.dtype == jnp.float32 else row[:heads] + row[heads : 2 * heads]
    return decay, message[:heads].astype(jnp.float32)


def paired_scan(decay, state, state_grad, axis, rider_fn, rider_inputs):
    peers = lax.axis_size(axis)
    if peers % 2:
        found = scanned_in([(decay, state, False), (decay, state_grad, True)], axis)
        return found[0], found[1], rider_fn(*rider_inputs)
    is_odd = lax.axis_index(axis) % 2 == 1
    swap = [(i, i ^ 1) for i in range(peers)]
    sent = jnp.where(is_odd, state_grad, state)
    message = packed(decay, sent, jnp.float32)
    if peers == 2:
        message, rider_inputs = lax.optimization_barrier((message, rider_inputs))
        riders = rider_fn(*rider_inputs)
    mate = lax.ppermute(message, axis, swap)
    if peers == 2:
        mate, riders = lax.optimization_barrier((mate, riders))
    mate_a, mate_s = unpacked(mate)
    own = jnp.where(is_odd, state, state_grad)
    window = (decay * mate_a, own + decay[:, None, None] * mate_s)
    near = (jnp.ones_like(decay), jnp.zeros_like(own))
    distance = 2
    while distance < peers:
        route = [(i, i + distance) for i in range(1, peers, 2) if i + distance < peers]
        route += [(i, i - distance) for i in range(0, peers, 2) if i - distance >= 0]
        if 2 * distance >= peers:
            far_s = lax.ppermute(window[1].astype(jnp.bfloat16), axis, route)
            if distance == 2:
                far_s, rider_inputs = lax.optimization_barrier((far_s, rider_inputs))
                riders = rider_fn(*rider_inputs)
            near = (near[0], near[1] + near[0][:, None, None] * far_s.astype(jnp.float32))
        else:
            far = lax.ppermute(packed(*window, jnp.bfloat16), axis, route)
            if distance == 2:
                far, rider_inputs = lax.optimization_barrier((far, rider_inputs))
                riders = rider_fn(*rider_inputs)
            far_a, far_s = unpacked(far)
            near = (near[0] * far_a, near[1] + near[0][:, None, None] * far_s)
            window = (window[0] * far_a, window[1] + window[0][:, None, None] * far_s)
        distance *= 2
    passing, riders = lax.optimization_barrier((near[1], riders))
    handed = lax.ppermute(passing, axis, swap)
    mine = mate_s + mate_a[:, None, None] * near[1]
    return jnp.where(is_odd, mine, handed), jnp.where(is_odd, handed, mine), riders


def shifted(block, axis, distance):
    devices = range(lax.axis_size(axis))
    route = [(i - distance, i) for i in devices if i - distance in devices]
    return lax.ppermute(block, axis, route)


def product(left, right):
    return jnp.dot(left, right, preferred_element_type=jnp.float32, precision=precise)


def body(
    conv_output, output_grad, write_keys, read_queries, log_decay, step_size, skip_gain, conv_weight
):
    length = conv_output.shape[0]
    head_count = log_decay.shape[1]
    head_width = conv_output.shape[1] // head_count
    parity = lax.axis_index("head") % 2
    own_first = parity == 0
    half = write_keys.shape[1]
    both = swapped(jnp.concatenate([write_keys, read_queries], 1), "head", 0)
    partner = (both[:, :half], both[:, half:])
    keys_full = jnp.where(
        own_first,
        jnp.concatenate([write_keys, partner[0]], 1),
        jnp.concatenate([partner[0], write_keys], 1),
    ).astype(jnp.float32)
    queries_full = jnp.where(
        own_first,
        jnp.concatenate([read_queries, partner[1]], 1),
        jnp.concatenate([partner[1], read_queries], 1),
    ).astype(jnp.float32)
    state_count = keys_full.shape[1]
    preact = conv_output.astype(jnp.float32)
    values = jax.nn.silu(preact)
    upstream = output_grad.astype(jnp.float32)
    values3 = values.reshape(length, head_count, head_width)
    upstream3 = upstream.reshape(length, head_count, head_width)
    token_row = lax.broadcasted_iota(jnp.int32, (length, length), 0)
    token_col = lax.broadcasted_iota(jnp.int32, (length, length), 1)
    cumulative = product((token_row >= token_col).astype(jnp.float32), log_decay)
    totals = cumulative[-1]
    to_end = jnp.exp(totals[None, :] - cumulative)
    from_start = jnp.exp(cumulative)
    weighted = values3 * (to_end * step_size)[:, :, None]
    seeded = upstream3 * from_start[:, :, None]
    def by_halves(own, other, mix):
        own_block = jnp.einsum("ln,lhp->hnp", own.astype(jnp.float32), mix, precision=precise)
        other_block = jnp.einsum("ln,lhp->hnp", other.astype(jnp.float32), mix, precision=precise)
        return jnp.where(
            own_first,
            jnp.concatenate([own_block, other_block], 1),
            jnp.concatenate([other_block, own_block], 1),
        )

    local_state = by_halves(write_keys, partner[0], weighted)
    local_grad = by_halves(read_queries, partner[1], seeded)
    decay_total = jnp.exp(totals)
    def local_terms(keys_full, queries_full, values3, upstream3, cumulative, step_size, preact):
        scores = product(queries_full, keys_full.T)
        row_ids = lax.broadcasted_iota(jnp.int32, (length, length), 0)
        col_ids = lax.broadcasted_iota(jnp.int32, (length, length), 1)
        causal = row_ids >= col_ids
        cum_heads = cumulative.T
        step_heads = step_size.T
        log_gap = jnp.where(causal[None], cum_heads[:, :, None] - cum_heads[:, None, :], -1e30)
        decay_mask = jnp.exp(log_gap)
        pair_dots = jnp.einsum("thp,shp->hts", upstream3, values3, precision=precise)
        masked_scores = decay_mask * scores[None]
        weight_sum = jnp.einsum("hts,hs->ts", decay_mask * pair_dots, step_heads, precision=precise)
        within = jnp.einsum(
            "hts,thp->shp", masked_scores * step_heads[:, None, :], upstream3, precision=precise
        )
        effect = masked_scores * pair_dots
        row_sums = jnp.einsum("hts,hs->th", effect, step_heads, precision=precise)
        col_sums = jnp.sum(effect, 1).T
        logistic = jax.nn.sigmoid(preact)
        return (
            within + skip_gain[None, :, None] * upstream3,
            row_sums - col_sums * step_size,
            col_sums,
            product(weight_sum, keys_full),
            lax.dot_general(
                weight_sum,
                queries_full,
                (((0,), (0,)), ((), ())),
                preferred_element_type=jnp.float32,
                precision=precise,
            ),
            logistic * (1.0 + preact * (1.0 - logistic)),
        )
    def local_block(*inputs):
        always = lax.axis_index("seq") >= 0
        return lax.cond(
            always,
            local_terms,
            lambda *a: jax.tree.map(jnp.zeros_like, local_terms(*a)),
            *inputs,
        )

    entering, arriving, riders = paired_scan(
        decay_total,
        local_state,
        local_grad,
        "seq",
        local_block,
        (keys_full, queries_full, values3, upstream3, cumulative, step_size, preact),
    )
    within_part, local_decay, col_sums, query_local, key_local, silu_slope = riders
    from_state = jnp.einsum("ln,hnp->lhp", queries_full, entering, precision=precise)
    into_state = jnp.einsum("ln,hnp->lhp", keys_full, arriving, precision=precise)
    carried = jnp.sum(values3 * into_state, 2)
    step_grad = col_sums + to_end * carried
    value_grad = within_part + (to_end * step_size)[:, :, None] * into_state
    leaving = decay_total[:, None, None] * entering + local_state
    decay_terms = (
        local_decay
        + from_start * jnp.sum(upstream3 * from_state, 2)
        - to_end * step_size * carried
    )
    last_row = (lax.broadcasted_iota(jnp.int32, (length, 1), 0) == length - 1).astype(jnp.float32)
    decay_terms = decay_terms + last_row * jnp.sum(arriving * leaving, (1, 2))[None, :]
    decay_grad = product((token_row <= token_col).astype(jnp.float32), decay_terms)
    query_part = query_local + jnp.einsum(
        "lhp,hnp->ln", seeded, entering, precision=precise
    )
    key_part = key_local + jnp.einsum("lhp,hnp->ln", weighted, arriving, precision=precise)
    half_width = state_count // 2
    key_mine = jnp.where(own_first, key_part[:, :half_width], key_part[:, half_width:])
    key_other = jnp.where(own_first, key_part[:, half_width:], key_part[:, :half_width])
    query_mine = jnp.where(own_first, query_part[:, :half_width], query_part[:, half_width:])
    query_other = jnp.where(own_first, query_part[:, half_width:], query_part[:, :half_width])
    sent_back = swapped(
        jnp.concatenate([key_other, query_other], 1).astype(jnp.bfloat16), "head", 0
    ).astype(key_other.dtype)
    received = (sent_back[:, :half_width], sent_back[:, half_width:])
    keys_grad = key_mine + received[0]
    queries_grad = query_mine + received[1]
    conv_grad = value_grad.reshape(length, -1) * silu_slope
    following = shifted(conv_grad[:3], "seq", -1)
    extended = jnp.concatenate([conv_grad, following], 0)
    input_grad = jnp.zeros_like(conv_grad)
    for offset in range(4):
        input_grad = (
            input_grad + conv_weight[offset][None, :] * extended[3 - offset : 3 - offset + length]
        )
    return (input_grad.astype(jnp.bfloat16), keys_grad, queries_grad, decay_grad, step_grad)


def solution(mesh):
    return jax.shard_map(
        body,
        mesh=mesh,
        in_specs=(
            P("seq", "head"),
            P("seq", "head"),
            P("seq", "head"),
            P("seq", "head"),
            P("seq", "head"),
            P("seq", "head"),
            P("head"),
            P(None, "head"),
        ),
        out_specs=(
            P("seq", "head"),
            P("seq", "head"),
            P("seq", "head"),
            P("seq", "head"),
            P("seq", "head"),
        ),
        check_vma=False,
    )
```

```python
import jax
import jax.numpy as jnp
from jax import lax
from jax.sharding import PartitionSpec as P

precise = lax.Precision.HIGHEST


def swapped(block, axis, bit):
    count = lax.axis_size(axis)
    route = []
    for low in range(count):
        high = low | 1 << bit
        if high != low and high < count:
            route += [(low, high), (high, low)]
    return lax.ppermute(block, axis, route)


def scanned_in(shards, axis):
    peers = lax.axis_size(axis)
    near = [(jnp.ones_like(a), jnp.zeros_like(s)) for a, s, _ in shards]
    window = [(a, s) for a, s, _ in shards]
    distance = 1
    while distance < peers:
        routes = []
        for _, _, reverse in shards:
            step = -distance if reverse else distance
            routes.append([(i, i + step) for i in range(peers) if 0 <= i + step < peers])
        received = [lax.ppermute(w, axis, r) for w, r in zip(window, routes)]
        more = 2 * distance < peers
        for k, (far_a, far_s) in enumerate(received):
            near_a, near_s = near[k]
            near[k] = (near_a * far_a, near_s + near_a[:, None, None] * far_s)
            if more:
                win_a, win_s = window[k]
                window[k] = (win_a * far_a, win_s + win_a[:, None, None] * far_s)
        distance *= 2
    return [s for _, s in near]


def packed(decay, state, kind):
    heads, width = state.shape[0], state.shape[1]
    if kind == jnp.float32:
        parts = decay
    else:
        high = decay.astype(kind)
        parts = jnp.concatenate([high, (decay - high.astype(decay.dtype)).astype(kind)])
    row = jnp.pad(parts.astype(kind), (0, width - parts.shape[0]))
    slab = jnp.broadcast_to(row[None, :, None], (1,) + state.shape[1:])
    return jnp.concatenate([state.astype(kind), slab], 0)


def unpacked(message):
    heads = message.shape[0] - 1
    row = message[heads, :, 0].astype(jnp.float32)
    decay = row[:heads] if message.dtype == jnp.float32 else row[:heads] + row[heads : 2 * heads]
    return decay, message[:heads].astype(jnp.float32)


def paired_scan(decay, state, state_grad, axis, rider_fn, rider_inputs):
    peers = lax.axis_size(axis)
    if peers % 2:
        found = scanned_in([(decay, state, False), (decay, state_grad, True)], axis)
        return found[0], found[1], rider_fn(*rider_inputs)
    is_odd = lax.axis_index(axis) % 2 == 1
    swap = [(i, i ^ 1) for i in range(peers)]
    sent = jnp.where(is_odd, state_grad, state)
    message = packed(decay, sent, jnp.float32)
    if peers == 2:
        message, rider_inputs = lax.optimization_barrier((message, rider_inputs))
        riders = rider_fn(*rider_inputs)
    mate = lax.ppermute(message, axis, swap)
    if peers == 2:
        mate, riders = lax.optimization_barrier((mate, riders))
    mate_a, mate_s = unpacked(mate)
    own = jnp.where(is_odd, state, state_grad)
    window = (decay * mate_a, own + decay[:, None, None] * mate_s)
    near = (jnp.ones_like(decay), jnp.zeros_like(own))
    distance = 2
    while distance < peers:
        route = [(i, i + distance) for i in range(1, peers, 2) if i + distance < peers]
        route += [(i, i - distance) for i in range(0, peers, 2) if i - distance >= 0]
        if 2 * distance >= peers:
            far_s = lax.ppermute(window[1].astype(jnp.bfloat16), axis, route)
            if distance == 2:
                far_s, rider_inputs = lax.optimization_barrier((far_s, rider_inputs))
                riders = rider_fn(*rider_inputs)
            near = (near[0], near[1] + near[0][:, None, None] * far_s.astype(jnp.float32))
        else:
            far = lax.ppermute(packed(*window, jnp.bfloat16), axis, route)
            if distance == 2:
                far, rider_inputs = lax.optimization_barrier((far, rider_inputs))
                riders = rider_fn(*rider_inputs)
            far_a, far_s = unpacked(far)
            near = (near[0] * far_a, near[1] + near[0][:, None, None] * far_s)
            window = (window[0] * far_a, window[1] + window[0][:, None, None] * far_s)
        distance *= 2
    passing, riders = lax.optimization_barrier((near[1], riders))
    handed = lax.ppermute(passing, axis, swap)
    mine = mate_s + mate_a[:, None, None] * near[1]
    return jnp.where(is_odd, mine, handed), jnp.where(is_odd, handed, mine), riders


def shifted(block, axis, distance):
    devices = range(lax.axis_size(axis))
    route = [(i - distance, i) for i in devices if i - distance in devices]
    return lax.ppermute(block, axis, route)


def product(left, right):
    return jnp.dot(left, right, preferred_element_type=jnp.float32, precision=precise)


def body(
    conv_output, output_grad, write_keys, read_queries, log_decay, step_size, skip_gain, conv_weight
):
    length = conv_output.shape[0]
    head_count = log_decay.shape[1]
    head_width = conv_output.shape[1] // head_count
    parity = lax.axis_index("head") % 2
    own_first = parity == 0
    half = write_keys.shape[1]
    both = swapped(jnp.concatenate([write_keys, read_queries], 1), "head", 0)
    partner = (both[:, :half], both[:, half:])
    keys_full = jnp.where(
        own_first,
        jnp.concatenate([write_keys, partner[0]], 1),
        jnp.concatenate([partner[0], write_keys], 1),
    ).astype(jnp.float32)
    queries_full = jnp.where(
        own_first,
        jnp.concatenate([read_queries, partner[1]], 1),
        jnp.concatenate([partner[1], read_queries], 1),
    ).astype(jnp.float32)
    state_count = keys_full.shape[1]
    preact = conv_output.astype(jnp.float32)
    values = jax.nn.silu(preact)
    upstream = output_grad.astype(jnp.float32)
    values3 = values.reshape(length, head_count, head_width)
    upstream3 = upstream.reshape(length, head_count, head_width)
    token_row = lax.broadcasted_iota(jnp.int32, (length, length), 0)
    token_col = lax.broadcasted_iota(jnp.int32, (length, length), 1)
    cumulative = product((token_row >= token_col).astype(jnp.float32), log_decay)
    totals = cumulative[-1]
    to_end = jnp.exp(totals[None, :] - cumulative)
    from_start = jnp.exp(cumulative)
    weighted = values3 * (to_end * step_size)[:, :, None]
    seeded = upstream3 * from_start[:, :, None]
    local_state = jnp.einsum("ln,lhp->hnp", keys_full, weighted, precision=precise)
    local_grad = jnp.einsum("ln,lhp->hnp", queries_full, seeded, precision=precise)
    decay_total = jnp.exp(totals)
    def local_terms(keys_full, queries_full, values3, upstream3, cumulative, step_size, preact):
        scores = product(queries_full, keys_full.T)
        row_ids = lax.broadcasted_iota(jnp.int32, (length, length), 0)
        col_ids = lax.broadcasted_iota(jnp.int32, (length, length), 1)
        causal = row_ids >= col_ids
        cum_heads = cumulative.T
        step_heads = step_size.T
        log_gap = jnp.where(causal[None], cum_heads[:, :, None] - cum_heads[:, None, :], -1e30)
        decay_mask = jnp.exp(log_gap)
        pair_dots = jnp.einsum("thp,shp->hts", upstream3, values3, precision=precise)
        masked_scores = decay_mask * scores[None]
        weight_sum = jnp.einsum("hts,hs->ts", decay_mask * pair_dots, step_heads, precision=precise)
        within = jnp.einsum(
            "hts,thp->shp", masked_scores * step_heads[:, None, :], upstream3, precision=precise
        )
        effect = masked_scores * pair_dots
        row_sums = jnp.einsum("hts,hs->th", effect, step_heads, precision=precise)
        col_sums = jnp.sum(effect, 1).T
        logistic = jax.nn.sigmoid(preact)
        return (
            within + skip_gain[None, :, None] * upstream3,
            row_sums - col_sums * step_size,
            col_sums,
            product(weight_sum, keys_full),
            lax.dot_general(
                weight_sum,
                queries_full,
                (((0,), (0,)), ((), ())),
                preferred_element_type=jnp.float32,
                precision=precise,
            ),
            logistic * (1.0 + preact * (1.0 - logistic)),
        )
    def local_block(*inputs):
        always = lax.axis_index("seq") >= 0
        return lax.cond(
            always,
            local_terms,
            lambda *a: jax.tree.map(jnp.zeros_like, local_terms(*a)),
            *inputs,
        )

    entering, arriving, riders = paired_scan(
        decay_total,
        local_state,
        local_grad,
        "seq",
        local_block,
        (keys_full, queries_full, values3, upstream3, cumulative, step_size, preact),
    )
    within_part, local_decay, col_sums, query_local, key_local, silu_slope = riders
    from_state = jnp.einsum("ln,hnp->lhp", queries_full, entering, precision=precise)
    into_state = jnp.einsum("ln,hnp->lhp", keys_full, arriving, precision=precise)
    carried = jnp.sum(values3 * into_state, 2)
    step_grad = col_sums + to_end * carried
    value_grad = within_part + (to_end * step_size)[:, :, None] * into_state
    leaving = decay_total[:, None, None] * entering + local_state
    decay_terms = (
        local_decay
        + from_start * jnp.sum(upstream3 * from_state, 2)
        - to_end * step_size * carried
    )
    last_row = (lax.broadcasted_iota(jnp.int32, (length, 1), 0) == length - 1).astype(jnp.float32)
    decay_terms = decay_terms + last_row * jnp.sum(arriving * leaving, (1, 2))[None, :]
    decay_grad = product((token_row <= token_col).astype(jnp.float32), decay_terms)
    query_part = query_local + jnp.einsum(
        "lhp,hnp->ln", seeded, entering, precision=precise
    )
    key_part = key_local + jnp.einsum("lhp,hnp->ln", weighted, arriving, precision=precise)
    half_width = state_count // 2
    key_mine = jnp.where(own_first, key_part[:, :half_width], key_part[:, half_width:])
    key_other = jnp.where(own_first, key_part[:, half_width:], key_part[:, :half_width])
    query_mine = jnp.where(own_first, query_part[:, :half_width], query_part[:, half_width:])
    query_other = jnp.where(own_first, query_part[:, half_width:], query_part[:, :half_width])
    key_mine, query_mine = lax.optimization_barrier((key_mine, query_mine))
    sent_back = swapped(
        jnp.concatenate([key_other, query_other], 1).astype(jnp.bfloat16), "head", 0
    ).astype(key_other.dtype)
    received = (sent_back[:, :half_width], sent_back[:, half_width:])
    keys_grad = key_mine + received[0]
    queries_grad = query_mine + received[1]
    conv_grad = value_grad.reshape(length, -1) * silu_slope
    following = shifted(conv_grad[:3], "seq", -1)
    extended = jnp.concatenate([conv_grad, following], 0)
    input_grad = jnp.zeros_like(conv_grad)
    for offset in range(4):
        input_grad = (
            input_grad + conv_weight[offset][None, :] * extended[3 - offset : 3 - offset + length]
        )
    return (input_grad.astype(jnp.bfloat16), keys_grad, queries_grad, decay_grad, step_grad)


def solution(mesh):
    return jax.shard_map(
        body,
        mesh=mesh,
        in_specs=(
            P("seq", "head"),
            P("seq", "head"),
            P("seq", "head"),
            P("seq", "head"),
            P("seq", "head"),
            P("seq", "head"),
            P("head"),
            P(None, "head"),
        ),
        out_specs=(
            P("seq", "head"),
            P("seq", "head"),
            P("seq", "head"),
            P("seq", "head"),
            P("seq", "head"),
        ),
        check_vma=False,
    )
```

```python
import jax
import jax.numpy as jnp
from jax import lax
from jax.sharding import PartitionSpec as P

precise = lax.Precision.HIGHEST


def swapped(block, axis, bit):
    count = lax.axis_size(axis)
    route = []
    for low in range(count):
        high = low | 1 << bit
        if high != low and high < count:
            route += [(low, high), (high, low)]
    return lax.ppermute(block, axis, route)


def scanned_in(shards, axis):
    peers = lax.axis_size(axis)
    near = [(jnp.ones_like(a), jnp.zeros_like(s)) for a, s, _ in shards]
    window = [(a, s) for a, s, _ in shards]
    distance = 1
    while distance < peers:
        routes = []
        for _, _, reverse in shards:
            step = -distance if reverse else distance
            routes.append([(i, i + step) for i in range(peers) if 0 <= i + step < peers])
        received = [lax.ppermute(w, axis, r) for w, r in zip(window, routes)]
        more = 2 * distance < peers
        for k, (far_a, far_s) in enumerate(received):
            near_a, near_s = near[k]
            near[k] = (near_a * far_a, near_s + near_a[:, None, None] * far_s)
            if more:
                win_a, win_s = window[k]
                window[k] = (win_a * far_a, win_s + win_a[:, None, None] * far_s)
        distance *= 2
    return [s for _, s in near]


def packed(decay, state, kind):
    heads, width = state.shape[0], state.shape[1]
    if kind == jnp.float32:
        parts = decay
    else:
        high = decay.astype(kind)
        parts = jnp.concatenate([high, (decay - high.astype(decay.dtype)).astype(kind)])
    row = jnp.pad(parts.astype(kind), (0, width - parts.shape[0]))
    slab = jnp.broadcast_to(row[None, :, None], (1,) + state.shape[1:])
    return jnp.concatenate([state.astype(kind), slab], 0)


def unpacked(message):
    heads = message.shape[0] - 1
    row = message[heads, :, 0].astype(jnp.float32)
    decay = row[:heads] if message.dtype == jnp.float32 else row[:heads] + row[heads : 2 * heads]
    return decay, message[:heads].astype(jnp.float32)


def paired_scan(decay, state, state_grad, axis, rider_fn, rider_inputs):
    peers = lax.axis_size(axis)
    if peers % 2:
        found = scanned_in([(decay, state, False), (decay, state_grad, True)], axis)
        return found[0], found[1], rider_fn(*rider_inputs)
    is_odd = lax.axis_index(axis) % 2 == 1
    swap = [(i, i ^ 1) for i in range(peers)]
    sent = jnp.where(is_odd, state_grad, state)
    message = packed(decay, sent, jnp.float32)
    if peers == 2:
        message, rider_inputs = lax.optimization_barrier((message, rider_inputs))
        riders = rider_fn(*rider_inputs)
    mate = lax.ppermute(message, axis, swap)
    if peers > 2:
        mate, rider_inputs = lax.optimization_barrier((mate, rider_inputs))
        riders = rider_fn(*rider_inputs)
    if peers == 2:
        mate, riders = lax.optimization_barrier((mate, riders))
    mate_a, mate_s = unpacked(mate)
    own = jnp.where(is_odd, state, state_grad)
    window = (decay * mate_a, own + decay[:, None, None] * mate_s)
    near = (jnp.ones_like(decay), jnp.zeros_like(own))
    distance = 2
    while distance < peers:
        route = [(i, i + distance) for i in range(1, peers, 2) if i + distance < peers]
        route += [(i, i - distance) for i in range(0, peers, 2) if i - distance >= 0]
        if 2 * distance >= peers:
            far_s = lax.ppermute(window[1].astype(jnp.bfloat16), axis, route)
            if distance == 2:
                far_s, riders = lax.optimization_barrier((far_s, riders))
            near = (near[0], near[1] + near[0][:, None, None] * far_s.astype(jnp.float32))
        else:
            far = lax.ppermute(packed(*window, jnp.bfloat16), axis, route)
            if distance == 2:
                far, riders = lax.optimization_barrier((far, riders))
            far_a, far_s = unpacked(far)
            near = (near[0] * far_a, near[1] + near[0][:, None, None] * far_s)
            window = (window[0] * far_a, window[1] + window[0][:, None, None] * far_s)
        distance *= 2
    passing, riders = lax.optimization_barrier((near[1], riders))
    handed = lax.ppermute(passing, axis, swap)
    mine = mate_s + mate_a[:, None, None] * near[1]
    return jnp.where(is_odd, mine, handed), jnp.where(is_odd, handed, mine), riders


def shifted(block, axis, distance):
    devices = range(lax.axis_size(axis))
    route = [(i - distance, i) for i in devices if i - distance in devices]
    return lax.ppermute(block, axis, route)


def product(left, right):
    return jnp.dot(left, right, preferred_element_type=jnp.float32, precision=precise)


def body(
    conv_output, output_grad, write_keys, read_queries, log_decay, step_size, skip_gain, conv_weight
):
    length = conv_output.shape[0]
    head_count = log_decay.shape[1]
    head_width = conv_output.shape[1] // head_count
    parity = lax.axis_index("head") % 2
    own_first = parity == 0
    half = write_keys.shape[1]
    both = swapped(jnp.concatenate([write_keys, read_queries], 1), "head", 0)
    partner = (both[:, :half], both[:, half:])
    keys_full = jnp.where(
        own_first,
        jnp.concatenate([write_keys, partner[0]], 1),
        jnp.concatenate([partner[0], write_keys], 1),
    ).astype(jnp.float32)
    queries_full = jnp.where(
        own_first,
        jnp.concatenate([read_queries, partner[1]], 1),
        jnp.concatenate([partner[1], read_queries], 1),
    ).astype(jnp.float32)
    state_count = keys_full.shape[1]
    preact = conv_output.astype(jnp.float32)
    values = jax.nn.silu(preact)
    upstream = output_grad.astype(jnp.float32)
    values3 = values.reshape(length, head_count, head_width)
    upstream3 = upstream.reshape(length, head_count, head_width)
    token_row = lax.broadcasted_iota(jnp.int32, (length, length), 0)
    token_col = lax.broadcasted_iota(jnp.int32, (length, length), 1)
    cumulative = product((token_row >= token_col).astype(jnp.float32), log_decay)
    totals = cumulative[-1]
    to_end = jnp.exp(totals[None, :] - cumulative)
    from_start = jnp.exp(cumulative)
    weighted = values3 * (to_end * step_size)[:, :, None]
    seeded = upstream3 * from_start[:, :, None]
    local_state = jnp.einsum("ln,lhp->hnp", keys_full, weighted, precision=precise)
    local_grad = jnp.einsum("ln,lhp->hnp", queries_full, seeded, precision=precise)
    decay_total = jnp.exp(totals)
    def local_terms(keys_full, queries_full, values3, upstream3, cumulative, step_size, preact):
        scores = product(queries_full, keys_full.T)
        row_ids = lax.broadcasted_iota(jnp.int32, (length, length), 0)
        col_ids = lax.broadcasted_iota(jnp.int32, (length, length), 1)
        causal = row_ids >= col_ids
        cum_heads = cumulative.T
        step_heads = step_size.T
        log_gap = jnp.where(causal[None], cum_heads[:, :, None] - cum_heads[:, None, :], -1e30)
        decay_mask = jnp.exp(log_gap)
        pair_dots = jnp.einsum("thp,shp->hts", upstream3, values3, precision=precise)
        masked_scores = decay_mask * scores[None]
        weight_sum = jnp.einsum("hts,hs->ts", decay_mask * pair_dots, step_heads, precision=precise)
        within = jnp.einsum(
            "hts,thp->shp", masked_scores * step_heads[:, None, :], upstream3, precision=precise
        )
        effect = masked_scores * pair_dots
        row_sums = jnp.einsum("hts,hs->th", effect, step_heads, precision=precise)
        col_sums = jnp.sum(effect, 1).T
        logistic = jax.nn.sigmoid(preact)
        return (
            within + skip_gain[None, :, None] * upstream3,
            row_sums - col_sums * step_size,
            col_sums,
            product(weight_sum, keys_full),
            lax.dot_general(
                weight_sum,
                queries_full,
                (((0,), (0,)), ((), ())),
                preferred_element_type=jnp.float32,
                precision=precise,
            ),
            logistic * (1.0 + preact * (1.0 - logistic)),
        )
    def local_block(*inputs):
        always = lax.axis_index("seq") >= 0
        return lax.cond(
            always,
            local_terms,
            lambda *a: jax.tree.map(jnp.zeros_like, local_terms(*a)),
            *inputs,
        )

    entering, arriving, riders = paired_scan(
        decay_total,
        local_state,
        local_grad,
        "seq",
        local_block,
        (keys_full, queries_full, values3, upstream3, cumulative, step_size, preact),
    )
    within_part, local_decay, col_sums, query_local, key_local, silu_slope = riders
    from_state = jnp.einsum("ln,hnp->lhp", queries_full, entering, precision=precise)
    into_state = jnp.einsum("ln,hnp->lhp", keys_full, arriving, precision=precise)
    carried = jnp.sum(values3 * into_state, 2)
    step_grad = col_sums + to_end * carried
    value_grad = within_part + (to_end * step_size)[:, :, None] * into_state
    leaving = decay_total[:, None, None] * entering + local_state
    decay_terms = (
        local_decay
        + from_start * jnp.sum(upstream3 * from_state, 2)
        - to_end * step_size * carried
    )
    last_row = (lax.broadcasted_iota(jnp.int32, (length, 1), 0) == length - 1).astype(jnp.float32)
    decay_terms = decay_terms + last_row * jnp.sum(arriving * leaving, (1, 2))[None, :]
    decay_grad = product((token_row <= token_col).astype(jnp.float32), decay_terms)
    query_part = query_local + jnp.einsum(
        "lhp,hnp->ln", seeded, entering, precision=precise
    )
    key_part = key_local + jnp.einsum("lhp,hnp->ln", weighted, arriving, precision=precise)
    half_width = state_count // 2
    key_mine = jnp.where(own_first, key_part[:, :half_width], key_part[:, half_width:])
    key_other = jnp.where(own_first, key_part[:, half_width:], key_part[:, :half_width])
    query_mine = jnp.where(own_first, query_part[:, :half_width], query_part[:, half_width:])
    query_other = jnp.where(own_first, query_part[:, half_width:], query_part[:, :half_width])
    sent_back = swapped(
        jnp.concatenate([key_other, query_other], 1).astype(jnp.bfloat16), "head", 0
    ).astype(key_other.dtype)
    received = (sent_back[:, :half_width], sent_back[:, half_width:])
    keys_grad = key_mine + received[0]
    queries_grad = query_mine + received[1]
    conv_grad = value_grad.reshape(length, -1) * silu_slope
    following = shifted(conv_grad[:3], "seq", -1)
    extended = jnp.concatenate([conv_grad, following], 0)
    input_grad = jnp.zeros_like(conv_grad)
    for offset in range(4):
        input_grad = (
            input_grad + conv_weight[offset][None, :] * extended[3 - offset : 3 - offset + length]
        )
    return (input_grad.astype(jnp.bfloat16), keys_grad, queries_grad, decay_grad, step_grad)


def solution(mesh):
    return jax.shard_map(
        body,
        mesh=mesh,
        in_specs=(
            P("seq", "head"),
            P("seq", "head"),
            P("seq", "head"),
            P("seq", "head"),
            P("seq", "head"),
            P("seq", "head"),
            P("head"),
            P(None, "head"),
        ),
        out_specs=(
            P("seq", "head"),
            P("seq", "head"),
            P("seq", "head"),
            P("seq", "head"),
            P("seq", "head"),
        ),
        check_vma=False,
    )
```
